128 devices in a mesh: gx: 8 (over y, z_lo), gy: 16 (over z_hi, x, core).
Axes of the slice: x: 4, y: 4, z: 4 (z_hi: 2, z_lo: 2; z = z_hi * 2 + z_lo), core: 2. Of those that a mesh axis runs over, the one named last changes fastest.
Arguments:
- right_side: float32 [3, 32, 128, 128], P(None, 'gx', 'gy'), may hold values from -8 to 8
- stiffness: float32 [32, 128, 128], P('gx', 'gy'), may hold values from 2.5 to 25
- panels: float32 [64, 3, 32, 128, 128], P(None, None, 'gx', 'gy'), may hold values from -0.21 to 0.21
Outputs:
- solution: float32 [3, 32, 128, 128], P(None, 'gx', 'gy')
- residual: float32 [3, 32, 128, 128], P(None, 'gx', 'gy')
- coupling: float32 [8, 16, 8, 4096], P('gx', 'gy')
The draws below stay inside these ranges and needn't reach their ends.
All inputs are finite; a program needn't handle non-finite values.
Results may differ from the reference program's by a relative error of at most 0.0003.
Values sent between devices are 32-bit elements; how exact they have to be, the bound alone decides.
No kernel may reach another device: no remote copies, remote signals or barrier semaphores. Data moves between devices by JAX's collectives and lax.ppermute only.
A program may use at most 192 MiB of HBM per device.

```python
import math
import jax
import jax.numpy as jnp
from jax import lax

CX = 4
CY = 8
CZ = 128
PANELS = 64
SWEEPS = 4
ITERS = 2
NX = 32
NY = 128
N_GX = 8
N_GY = 16


def spread_blocks(values):
    widened = jnp.repeat(values, CX, axis=2, total_repeat_length=NX)
    return jnp.repeat(widened, CY, axis=3, total_repeat_length=NY)


def draw_panels(key, part):
    key_list = jax.random.split(jax.random.fold_in(key, 11), 9)
    block_grid = (PANELS, 3, NX // CX, NY // CY)
    panel_order = jnp.arange(PANELS, dtype=jnp.int32)
    mode_first = (panel_order % 4).astype(jnp.float32)[:, None, None, None]
    mode_second = (panel_order // 4 % 4).astype(jnp.float32)[:, None, None, None]
    mode_third = (panel_order // 16 % 4).astype(jnp.float32)[:, None, None, None]
    freq_first = spread_blocks(mode_first + jax.random.uniform(key_list[0], block_grid, jnp.float32, 0.0, 0.6))
    freq_second = spread_blocks(mode_second + jax.random.uniform(key_list[1], block_grid, jnp.float32, 0.0, 0.6))
    freq_third = spread_blocks(mode_third + jax.random.uniform(key_list[2], block_grid, jnp.float32, 0.0, 0.6))
    phase_first = spread_blocks(jax.random.uniform(key_list[3], block_grid, jnp.float32, -0.5, 0.5))
    phase_second = spread_blocks(jax.random.uniform(key_list[4], block_grid, jnp.float32, -0.5, 0.5))
    phase_third = spread_blocks(jax.random.uniform(key_list[5], block_grid, jnp.float32, -0.5, 0.5))
    full_shape = (PANELS, 3, NX, NY, CZ)
    magnitude = jnp.exp(jax.random.uniform(key_list[6], block_grid, jnp.float32, math.log(0.5), math.log(1.6)))
    rough_part = 0.15 * jax.random.truncated_normal(key_list[8], -3.0, 3.0, full_shape, jnp.float32)
    sign_values = (2 * jax.random.randint(key_list[7], block_grid, 0, 2) - 1).astype(jnp.float32)
    amplitude = spread_blocks(magnitude * sign_values)
    local_first = ((jnp.arange(NX) % CX).astype(jnp.float32) + 0.5) / CX
    local_second = ((jnp.arange(NY) % CY).astype(jnp.float32) + 0.5) / CY
    local_third = (jnp.arange(CZ).astype(jnp.float32) + 0.5) / CZ
    wave_first = jnp.cos(math.pi * (freq_first * local_first[:, None] + phase_first))
    wave_second = jnp.cos(math.pi * (freq_second * local_second[None, :] + phase_second))
    wave_third = jnp.cos(math.pi * (freq_third[..., None] * local_third + phase_third[..., None]))
    smooth_part = (amplitude * wave_first * wave_second)[..., None] * wave_third
    return (0.09 * (smooth_part + rough_part)).astype(jnp.float32)


def draw_right_side(key, part):
    key_list = jax.random.split(jax.random.fold_in(key, 23), 9)
    full_shape = (3, NX, NY, CZ)
    comp_shape = (3, 1, 1, 1)
    coord_first = ((jnp.arange(NX).astype(jnp.float32) + 0.5) / NX)[:, None, None]
    coord_second = ((jnp.arange(NY).astype(jnp.float32) + 0.5) / NY)[None, :, None]
    coord_third = (jnp.arange(CZ).astype(jnp.float32) + 0.5) / CZ
    freq_first = jax.random.uniform(key_list[0], comp_shape, jnp.float32, 0.5, 1.5)
    freq_second = jax.random.uniform(key_list[1], comp_shape, jnp.float32, 0.5, 1.5)
    freq_third = jax.random.uniform(key_list[2], comp_shape, jnp.float32, 0.5, 1.5)
    phase_first = jax.random.uniform(key_list[3], comp_shape, jnp.float32, -0.3, 0.3)
    phase_second = jax.random.uniform(key_list[4], comp_shape, jnp.float32, -0.3, 0.3)
    phase_third = jax.random.uniform(key_list[5], comp_shape, jnp.float32, -0.3, 0.3)
    wave_field = jnp.cos(math.pi * (freq_first * coord_first + phase_first))
    wave_field = wave_field * jnp.cos(math.pi * (freq_second * coord_second + phase_second))
    wave_field = wave_field * jnp.cos(math.pi * (freq_third * coord_third + phase_third))
    base_level = jax.random.uniform(key_list[6], comp_shape, jnp.float32, -0.8, 0.8)
    swing_size = jax.random.uniform(key_list[7], comp_shape, jnp.float32, 0.5, 1.0)
    rough_part = jax.random.truncated_normal(key_list[8], -6.0, 6.0, full_shape, jnp.float32)
    return (base_level + swing_size * wave_field + rough_part).astype(jnp.float32)


def block_levels(rng, extent, shards, low, top_value):
    loudness, own = 1.0, jax.random.fold_in(rng, 6)
    for dim, shards_of in shards:
        draws = jnp.exp(jax.random.uniform(jax.random.fold_in(own, dim), (shards_of,), jnp.float32, low / len(shards), top_value / len(shards)))
        loudness = loudness * jnp.repeat(draws, extent[dim] // shards_of).reshape([-1 if axis == dim else 1 for axis in range(len(extent))])
    return loudness


def setup_inputs(seed: int = 0) -> dict:
    splits = jax.random.split(jax.random.key(seed), 4)
    return {
        "right_side": draw_right_side(jax.random.fold_in(splits[3], 71), 0),
        "stiffness": jnp.clip(jnp.exp(math.log(25.0) - 2.3025851 * jax.random.uniform(splits[1], (NX, NY, CZ), jnp.float32) ** block_levels(splits[1], (NX, NY, CZ), ((0, 8), (1, 16)), -0.2, 0.2)), 2.5, 25.0),
        "panels": draw_panels(jax.random.fold_in(splits[3], 71), 0),
    }


precise = lax.Precision.HIGHEST
mixing = 0.25
damping = 0.5
neighbours = ((-1, -1), (-1, 0), (-1, 1), (0, -1), (0, 1), (1, -1), (1, 0), (1, 1))


def apply_stencil(window, stiff_block):
    paddings = [(0, 0)] * (window.ndim - 1) + [(1, 1)]
    widened = jnp.pad(window, paddings)
    along_first = widened[..., :-2, :, :] + widened[..., 1:-1, :, :] + widened[..., 2:, :, :]
    along_second = along_first[..., :, :-2, :] + along_first[..., :, 1:-1, :] + along_first[..., :, 2:, :]
    box_sum = along_second[..., :-2] + along_second[..., 1:-1] + along_second[..., 2:]
    centre = window[..., 1:-1, 1:-1, :]
    slope_first = widened[..., 2:, :, :] - widened[..., :-2, :, :]
    slope_second = widened[..., 1:-1, 2:, :] - widened[..., 1:-1, :-2, :]
    mixed_ab = slope_first[..., :, 2:, 1:-1] - slope_first[..., :, :-2, 1:-1]
    mixed_ac = slope_first[..., :, 1:-1, 2:] - slope_first[..., :, 1:-1, :-2]
    mixed_bc = slope_second[..., 2:] - slope_second[..., :-2]
    cross_terms = jnp.stack([
        mixed_ab[..., 1, :, :, :] + mixed_ac[..., 2, :, :, :],
        mixed_ab[..., 0, :, :, :] + mixed_bc[..., 2, :, :, :],
        mixed_ac[..., 0, :, :, :] + mixed_bc[..., 1, :, :, :]], axis=-4)
    return (27.0 + stiff_block) * centre - box_sum + mixing * cross_terms


def window_plan(offset, length):
    if offset == 0:
        return (0, length + 2, 1, length + 1, 0, length)
    if offset == 1:
        return (length - 1, length + 2, 2, 3, length - 1, length)
    return (0, 3, 0, 1, 0, 1)


def select_mask(plan):
    places = jnp.arange(plan[1] - plan[0])
    return ((places >= plan[2]) & (places < plan[3])).astype(jnp.float32)


def coarse_tile(padded, own_panels, stiff_block, shift_first, shift_second):
    plan_first = window_plan(shift_first, own_panels.shape[2])
    plan_second = window_plan(shift_second, own_panels.shape[3])
    window = padded[:, :, plan_first[0]:plan_first[1], plan_second[0]:plan_second[1], :]
    keep_first = select_mask(plan_first)
    keep_second = select_mask(plan_second)
    masked = window * (keep_first[:, None, None] * keep_second[None, :, None])
    imaged = apply_stencil(masked, stiff_block[plan_first[4]:plan_first[5], plan_second[4]:plan_second[5], :])
    panel_part = own_panels[:, :, plan_first[4]:plan_first[5], plan_second[4]:plan_second[5], :]
    return jnp.einsum("kabcd,labcd->kl", panel_part, imaged, precision=precise)


def jacobi(ext_residual, ext_stiff):
    inv_diag = damping / (26.0 + ext_stiff)
    correction = inv_diag * ext_residual
    for sweep_index in range(SWEEPS - 1):
        widened = jnp.pad(correction, ((0, 0), (1, 1), (1, 1), (0, 0)))
        correction = correction + inv_diag * (ext_residual - apply_stencil(widened, ext_stiff))
    return correction


def reference(right_side, stiffness, panels):
    anchor = jnp.int32(0)
    block_ids = jnp.arange(N_GX * N_GY, dtype=jnp.int32)
    panels_wide = jnp.pad(panels, ((0, 0), (0, 0), (1, 1), (1, 1), (0, 0)))
    stiff_wide = jnp.pad(stiffness, ((1, 1), (1, 1), (0, 0)))

    def block_tiles(block_index):
        block_row = block_index // N_GY
        block_column = block_index % N_GY
        padded = lax.dynamic_slice(panels_wide, (anchor, anchor, block_row * CX, block_column * CY, anchor), (PANELS, 3, CX + 2, CY + 2, CZ))
        stiff_block = lax.dynamic_slice(stiffness, (block_row * CX, block_column * CY, anchor), (CX, CY, CZ))
        own_panels = padded[:, :, 1:-1, 1:-1, :]
        diag_tile = coarse_tile(padded, own_panels, stiff_block, 0, 0)
        others = jnp.stack([coarse_tile(padded, own_panels, stiff_block, shift_first, shift_second) for shift_first, shift_second in neighbours])
        return diag_tile, others

    diag_all, coupling_all = lax.map(block_tiles, block_ids)
    diag_all = diag_all.reshape(N_GX, N_GY, PANELS, PANELS)
    coupling_all = coupling_all.reshape(N_GX, N_GY, 8, PANELS, PANELS)
    weights = damping / jnp.diagonal(diag_all, axis1=2, axis2=3)
    panels_view = panels.reshape(PANELS, 3, N_GX, CX, N_GY, CY, CZ)

    def coarse_times(vector):
        vector_wide = jnp.pad(vector, ((1, 1), (1, 1), (0, 0)))
        totals = jnp.einsum("ghkl,ghl->ghk", diag_all, vector, precision=precise)
        for place, (shift_first, shift_second) in enumerate(neighbours):
            shifted = vector_wide[1 + shift_first:1 + shift_first + N_GX, 1 + shift_second:1 + shift_second + N_GY]
            totals = totals + jnp.einsum("ghkl,ghl->ghk", coupling_all[:, :, place], shifted, precision=precise)
        return totals

    def precondition(current):
        current_view = current.reshape(3, N_GX, CX, N_GY, CY, CZ)
        restricted = jnp.einsum("kagchdz,agchdz->ghk", panels_view, current_view, precision=precise)
        first_guess = weights * restricted
        coarse_vec = first_guess + weights * (restricted - coarse_times(first_guess))
        coarse_part = jnp.einsum("kagchdz,ghk->agchdz", panels_view, coarse_vec, precision=precise).reshape(3, NX, NY, CZ)
        current_wide = jnp.pad(current, ((0, 0), (1, 1), (1, 1), (0, 0)))

        def local_block(block_index):
            block_row = block_index // N_GY
            block_column = block_index % N_GY
            ext_residual = lax.dynamic_slice(current_wide, (anchor, block_row * CX, block_column * CY, anchor), (3, CX + 2, CY + 2, CZ))
            ext_stiff = lax.dynamic_slice(stiff_wide, (block_row * CX, block_column * CY, anchor), (CX + 2, CY + 2, CZ))
            return jacobi(ext_residual, ext_stiff)

        pieces = lax.map(local_block, block_ids)

        def accumulate(counter, summed):
            block_index = jnp.asarray(counter).astype(jnp.int32)
            block_row = block_index // N_GY
            block_column = block_index % N_GY
            starts = (anchor, block_row * CX, block_column * CY, anchor)
            present = lax.dynamic_slice(summed, starts, (3, CX + 2, CY + 2, CZ))
            return lax.dynamic_update_slice(summed, present + pieces[block_index], starts)

        summed = lax.fori_loop(0, N_GX * N_GY, accumulate, jnp.zeros((3, NX + 2, NY + 2, CZ), jnp.float32))
        return summed[:, 1:-1, 1:-1, :] + coarse_part

    def operate(field_in):
        return apply_stencil(jnp.pad(field_in, ((0, 0), (1, 1), (1, 1), (0, 0))), stiffness)

    solution = jnp.zeros_like(right_side)
    residual = right_side
    precond = precondition(residual)
    direction = precond
    fit_now = jnp.sum(residual * precond)
    for iteration in range(ITERS):
        imaged = operate(direction)
        step_size = fit_now / jnp.sum(direction * imaged)
        solution = solution + step_size * direction
        residual = residual - step_size * imaged
        if iteration + 1 < ITERS:
            precond = precondition(residual)
            fit_next = jnp.sum(residual * precond)
            direction = precond + (fit_next / fit_now) * direction
            fit_now = fit_next
    coupling = coupling_all.reshape(N_GX, N_GY, 8, PANELS * PANELS)
    return (solution, residual, coupling)
```

```python
import jax
import jax.numpy as jnp
from jax import lax
from jax.sharding import PartitionSpec as P

SWEEPS = 4
ITERS = 2


precise = lax.Precision.HIGHEST
mixing = 0.25
damping = 0.5
neighbours = ((-1, -1), (-1, 0), (-1, 1), (0, -1), (0, 1), (1, -1), (1, 0), (1, 1))


def with_halo(value, sides, width):
    for axis, dim in sides:
        size, length = (lax.axis_size(axis), value.shape[dim])
        up = [(i, (i + 1) % size) for i in range(size - 1)]
        down = [(j, i) for i, j in up]
        last = lax.slice_in_dim(value, length - width, length, axis=dim)
        initial = lax.slice_in_dim(value, 0, width, axis=dim)
        before = lax.ppermute(last, axis, up)
        after = lax.ppermute(initial, axis, down)
        value = jnp.concatenate([before, value, after], axis=dim)
    return value


def butterfly_sum(value, axes):
    for axis in axes:
        size = lax.axis_size(axis)
        stride = 1
        while stride < size:
            partners = [(i, i ^ stride) for i in range(size)]
            value = value + lax.ppermute(value, axis, partners)
            stride *= 2
    return value


def apply_stencil(window, stiff_block):
    paddings = [(0, 0)] * (window.ndim - 1) + [(1, 1)]
    widened = jnp.pad(window, paddings)
    along_first = widened[..., :-2, :, :] + widened[..., 1:-1, :, :] + widened[..., 2:, :, :]
    along_second = (
        along_first[..., :, :-2, :] + along_first[..., :, 1:-1, :] + along_first[..., :, 2:, :]
    )
    box_sum = along_second[..., :-2] + along_second[..., 1:-1] + along_second[..., 2:]
    centre = window[..., 1:-1, 1:-1, :]
    slope_first = widened[..., 2:, :, :] - widened[..., :-2, :, :]
    slope_second = widened[..., 1:-1, 2:, :] - widened[..., 1:-1, :-2, :]
    mixed_ab = slope_first[..., :, 2:, 1:-1] - slope_first[..., :, :-2, 1:-1]
    mixed_ac = slope_first[..., :, 1:-1, 2:] - slope_first[..., :, 1:-1, :-2]
    mixed_bc = slope_second[..., 2:] - slope_second[..., :-2]
    cross_terms = jnp.stack(
        [
            mixed_ab[..., 1, :, :, :] + mixed_ac[..., 2, :, :, :],
            mixed_ab[..., 0, :, :, :] + mixed_bc[..., 2, :, :, :],
            mixed_ac[..., 0, :, :, :] + mixed_bc[..., 1, :, :, :],
        ],
        axis=-4,
    )
    return (27.0 + stiff_block) * centre - box_sum + mixing * cross_terms


def window_plan(offset, length):
    if offset == 0:
        return (0, length + 2, 1, length + 1, 0, length)
    if offset == 1:
        return (length - 1, length + 2, 2, 3, length - 1, length)
    return (0, 3, 0, 1, 0, 1)


def select_mask(plan):
    places = jnp.arange(plan[1] - plan[0])
    return ((places >= plan[2]) & (places < plan[3])).astype(jnp.float32)


def coarse_tile(padded, own_panels, stiff_block, shift_first, shift_second):
    plan_first = window_plan(shift_first, own_panels.shape[2])
    plan_second = window_plan(shift_second, own_panels.shape[3])
    window = padded[:, :, plan_first[0] : plan_first[1], plan_second[0] : plan_second[1], :]
    keep_first = select_mask(plan_first)
    keep_second = select_mask(plan_second)
    masked = window * (keep_first[:, None, None] * keep_second[None, :, None])
    imaged = apply_stencil(
        masked, stiff_block[plan_first[4] : plan_first[5], plan_second[4] : plan_second[5], :]
    )
    panel_part = own_panels[:, :, plan_first[4] : plan_first[5], plan_second[4] : plan_second[5], :]
    return jnp.einsum("kabcd,labcd->kl", panel_part, imaged, precision=precise)


def jacobi(ext_residual, ext_stiff):
    inv_diag = damping / (26.0 + ext_stiff)
    correction = inv_diag * ext_residual
    for sweep_index in range(SWEEPS - 1):
        widened = jnp.pad(correction, ((0, 0), (1, 1), (1, 1), (0, 0)))
        correction = correction + inv_diag * (ext_residual - apply_stencil(widened, ext_stiff))
    return correction


def fold_axis(spread, dimension, length):
    interior = lax.slice_in_dim(spread, 2, 2 + length, axis=dimension)
    lower_part = lax.slice_in_dim(spread, 0, 1, axis=dimension)
    upper_part = lax.slice_in_dim(spread, length + 3, length + 4, axis=dimension)
    pads_low = [(0, 0)] * spread.ndim
    pads_high = [(0, 0)] * spread.ndim
    pads_low[dimension] = (0, length - 1)
    pads_high[dimension] = (length - 1, 0)
    return interior + jnp.pad(lower_part, pads_low) + jnp.pad(upper_part, pads_high)


def per_device(right_side, stiffness, panels):
    cells_first = stiffness.shape[0]
    cells_second = stiffness.shape[1]
    padded, stiff_wide = (
        with_halo(panels, (("gx", 2), ("gy", 3)), 1),
        with_halo(stiffness[None, None], (("gx", 2), ("gy", 3)), 1),
    )
    ext_stiff = stiff_wide[0, 0]
    diag_tile = coarse_tile(padded, panels, stiffness, 0, 0)
    tile_list = [
        coarse_tile(padded, panels, stiffness, shift_first, shift_second)
        for shift_first, shift_second in neighbours
    ]
    weights = damping / jnp.diagonal(diag_tile)

    def precondition(current):
        restricted = jnp.einsum("kabcd,abcd->k", panels, current, precision=precise)
        first_guess = weights * restricted
        nearby = with_halo(first_guess[None, None], (("gx", 0), ("gy", 1)), 1)
        applied = jnp.dot(diag_tile, first_guess, precision=precise)
        for place, (shift_first, shift_second) in enumerate(neighbours):
            applied = applied + jnp.dot(
                tile_list[place], nearby[1 + shift_first, 1 + shift_second], precision=precise
            )
        coarse_vec = first_guess + weights * (restricted - applied)
        coarse_part = jnp.einsum("k,kabcd->abcd", coarse_vec, panels, precision=precise)
        ext_residual = with_halo(current, (("gx", 1), ("gy", 2)), 1)
        correction = jacobi(ext_residual, ext_stiff)
        spread = with_halo(correction, (("gx", 1), ("gy", 2)), 1)
        folded = fold_axis(fold_axis(spread, 1, cells_first), 2, cells_second)
        return folded + coarse_part

    def inner_fit(current, precond):
        return butterfly_sum(jnp.sum(current * precond), ("gx", "gy"))

    solution = jnp.zeros_like(right_side)
    residual = right_side
    precond = precondition(residual)
    direction = precond
    fit_local = jnp.sum(residual * precond)
    fit_now = None
    for iteration in range(ITERS):
        widened = with_halo(direction, (("gx", 1), ("gy", 2)), 1)
        imaged = apply_stencil(widened, stiffness)
        curve_local = jnp.sum(direction * imaged)
        if fit_now is None:
            both = butterfly_sum(jnp.stack([fit_local, curve_local]), ("gx", "gy"))
            fit_now, curve = both[0], both[1]
        else:
            curve = butterfly_sum(curve_local, ("gx", "gy"))
        step_size = fit_now / curve
        solution = solution + step_size * direction
        residual = residual - step_size * imaged
        if iteration + 1 < ITERS:
            precond = precondition(residual)
            fit_next = inner_fit(residual, precond)
            direction = precond + fit_next / fit_now * direction
            fit_now = fit_next
    coupling = jnp.stack(tile_list).reshape(1, 1, 8, -1)
    return (solution, residual, coupling)


def solution(mesh):
    return jax.shard_map(
        per_device,
        mesh=mesh,
        in_specs=(P(None, "gx", "gy", None), P("gx", "gy", None), P(None, None, "gx", "gy", None)),
        out_specs=(P(None, "gx", "gy", None), P(None, "gx", "gy", None), P("gx", "gy", None, None)),
        check_vma=False,
    )
```

```python
import jax
import jax.numpy as jnp
from jax import lax
from jax.sharding import PartitionSpec as P

SWEEPS = 4
ITERS = 2


precise = lax.Precision.HIGHEST
mixing = 0.25
damping = 0.5
neighbours = ((-1, -1), (-1, 0), (-1, 1), (0, -1), (0, 1), (1, -1), (1, 0), (1, 1))


def with_halo(value, sides, width):
    for axis, dim in sides:
        size, length = (lax.axis_size(axis), value.shape[dim])
        up = [(i, (i + 1) % size) for i in range(size - 1)]
        down = [(j, i) for i, j in up]
        last = lax.slice_in_dim(value, length - width, length, axis=dim)
        initial = lax.slice_in_dim(value, 0, width, axis=dim)
        before = lax.ppermute(last, axis, up)
        after = lax.ppermute(initial, axis, down)
        value = jnp.concatenate([before, value, after], axis=dim)
    return value


def butterfly_sum(value, axes):
    for axis in axes:
        size = lax.axis_size(axis)
        stride = 1
        while stride < size:
            partners = [(i, i ^ stride) for i in range(size)]
            value = value + lax.ppermute(value, axis, partners)
            stride *= 2
    return value


def apply_stencil(window, stiff_block):
    paddings = [(0, 0)] * (window.ndim - 1) + [(1, 1)]
    widened = jnp.pad(window, paddings)
    along_first = widened[..., :-2, :, :] + widened[..., 1:-1, :, :] + widened[..., 2:, :, :]
    along_second = (
        along_first[..., :, :-2, :] + along_first[..., :, 1:-1, :] + along_first[..., :, 2:, :]
    )
    box_sum = along_second[..., :-2] + along_second[..., 1:-1] + along_second[..., 2:]
    centre = window[..., 1:-1, 1:-1, :]
    slope_first = widened[..., 2:, :, :] - widened[..., :-2, :, :]
    slope_second = widened[..., 1:-1, 2:, :] - widened[..., 1:-1, :-2, :]
    mixed_ab = slope_first[..., :, 2:, 1:-1] - slope_first[..., :, :-2, 1:-1]
    mixed_ac = slope_first[..., :, 1:-1, 2:] - slope_first[..., :, 1:-1, :-2]
    mixed_bc = slope_second[..., 2:] - slope_second[..., :-2]
    cross_terms = jnp.stack(
        [
            mixed_ab[..., 1, :, :, :] + mixed_ac[..., 2, :, :, :],
            mixed_ab[..., 0, :, :, :] + mixed_bc[..., 2, :, :, :],
            mixed_ac[..., 0, :, :, :] + mixed_bc[..., 1, :, :, :],
        ],
        axis=-4,
    )
    return (27.0 + stiff_block) * centre - box_sum + mixing * cross_terms


def window_plan(offset, length):
    if offset == 0:
        return (0, length + 2, 1, length + 1, 0, length)
    if offset == 1:
        return (length - 1, length + 2, 2, 3, length - 1, length)
    return (0, 3, 0, 1, 0, 1)


def select_mask(plan):
    places = jnp.arange(plan[1] - plan[0])
    return ((places >= plan[2]) & (places < plan[3])).astype(jnp.float32)


def coarse_tile(padded, own_panels, stiff_block, shift_first, shift_second):
    plan_first = window_plan(shift_first, own_panels.shape[2])
    plan_second = window_plan(shift_second, own_panels.shape[3])
    window = padded[:, :, plan_first[0] : plan_first[1], plan_second[0] : plan_second[1], :]
    keep_first = select_mask(plan_first)
    keep_second = select_mask(plan_second)
    masked = window * (keep_first[:, None, None] * keep_second[None, :, None])
    imaged = apply_stencil(
        masked, stiff_block[plan_first[4] : plan_first[5], plan_second[4] : plan_second[5], :]
    )
    panel_part = own_panels[:, :, plan_first[4] : plan_first[5], plan_second[4] : plan_second[5], :]
    return jnp.einsum("kabcd,labcd->kl", panel_part, imaged, precision=precise)


def jacobi(ext_residual, ext_stiff):
    inv_diag = damping / (26.0 + ext_stiff)
    correction = inv_diag * ext_residual
    for sweep_index in range(SWEEPS - 1):
        widened = jnp.pad(correction, ((0, 0), (1, 1), (1, 1), (0, 0)))
        correction = correction + inv_diag * (ext_residual - apply_stencil(widened, ext_stiff))
    return correction


def fold_axis(spread, dimension, length):
    interior = lax.slice_in_dim(spread, 2, 2 + length, axis=dimension)
    lower_part = lax.slice_in_dim(spread, 0, 1, axis=dimension)
    upper_part = lax.slice_in_dim(spread, length + 3, length + 4, axis=dimension)
    pads_low = [(0, 0)] * spread.ndim
    pads_high = [(0, 0)] * spread.ndim
    pads_low[dimension] = (0, length - 1)
    pads_high[dimension] = (length - 1, 0)
    return interior + jnp.pad(lower_part, pads_low) + jnp.pad(upper_part, pads_high)


def per_device(right_side, stiffness, panels):
    cells_first = stiffness.shape[0]
    cells_second = stiffness.shape[1]
    padded, stiff_wide = (
        with_halo(panels, (("gx", 2), ("gy", 3)), 1),
        with_halo(stiffness[None, None], (("gx", 2), ("gy", 3)), 1),
    )
    ext_stiff = stiff_wide[0, 0]
    diag_tile = coarse_tile(padded, panels, stiffness, 0, 0)
    tile_list = [
        coarse_tile(padded, panels, stiffness, shift_first, shift_second)
        for shift_first, shift_second in neighbours
    ]
    weights = damping / jnp.diagonal(diag_tile)

    def precondition(current):
        restricted = jnp.einsum("kabcd,abcd->k", panels, current, precision=precise)
        first_guess = weights * restricted
        nearby = with_halo(first_guess[None, None], (("gx", 0), ("gy", 1)), 1)
        applied = jnp.dot(diag_tile, first_guess, precision=precise)
        for place, (shift_first, shift_second) in enumerate(neighbours):
            applied = applied + jnp.dot(
                tile_list[place], nearby[1 + shift_first, 1 + shift_second], precision=precise
            )
        coarse_vec = first_guess + weights * (restricted - applied)
        coarse_part = jnp.einsum("k,kabcd->abcd", coarse_vec, panels, precision=precise)
        ext_residual = with_halo(current, (("gx", 1), ("gy", 2)), 1)
        correction = jacobi(ext_residual, ext_stiff)
        spread = with_halo(correction, (("gx", 1), ("gy", 2)), 1)
        folded = fold_axis(fold_axis(spread, 1, cells_first), 2, cells_second)
        return folded + coarse_part

    def operate(field):
        return apply_stencil(with_halo(field, (("gx", 1), ("gy", 2)), 1), stiffness)

    residual = right_side
    precond = precondition(residual)
    imaged = operate(precond)
    smoothed = precondition(imaged)
    twice = operate(smoothed)
    local_dots = jnp.stack(
        [
            jnp.sum(residual * precond),
            jnp.sum(precond * imaged),
            jnp.sum(residual * smoothed),
            jnp.sum(imaged * smoothed),
            jnp.sum(precond * twice),
            jnp.sum(smoothed * twice),
        ]
    )
    fit, curve, cross_r, cross_q, cross_z, curve_w = butterfly_sum(local_dots, ("gx", "gy"))
    step_first = fit / curve
    solution = step_first * precond
    residual = residual - step_first * imaged
    fit_next = fit - step_first * (curve + cross_r) + step_first * step_first * cross_q
    ratio = fit_next / fit
    grown = 1.0 + ratio
    curve_next = (
        grown * grown * curve
        - step_first * grown * (cross_z + cross_q)
        + step_first * step_first * curve_w
    )
    step_second = fit_next / curve_next
    precond_next = precond - step_first * smoothed
    direction = precond_next + ratio * precond
    imaged_next = (imaged - step_first * twice) + ratio * imaged
    solution = solution + step_second * direction
    residual = residual - step_second * imaged_next
    coupling = jnp.stack(tile_list).reshape(1, 1, 8, -1)
    return (solution, residual, coupling)


def solution(mesh):
    return jax.shard_map(
        per_device,
        mesh=mesh,
        in_specs=(P(None, "gx", "gy", None), P("gx", "gy", None), P(None, None, "gx", "gy", None)),
        out_specs=(P(None, "gx", "gy", None), P(None, "gx", "gy", None), P("gx", "gy", None, None)),
        check_vma=False,
    )
```

```python
import jax
import jax.numpy as jnp
from jax import lax
from jax.sharding import PartitionSpec as P

SWEEPS = 4
ITERS = 2


precise = lax.Precision.HIGHEST
mixing = 0.25
damping = 0.5
neighbours = ((-1, -1), (-1, 0), (-1, 1), (0, -1), (0, 1), (1, -1), (1, 0), (1, 1))


def with_halo(value, sides, width):
    for axis, dim in sides:
        size, length = (lax.axis_size(axis), value.shape[dim])
        up = [(i, (i + 1) % size) for i in range(size - 1)]
        down = [(j, i) for i, j in up]
        last = lax.slice_in_dim(value, length - width, length, axis=dim)
        initial = lax.slice_in_dim(value, 0, width, axis=dim)
        before = lax.ppermute(last, axis, up)
        after = lax.ppermute(initial, axis, down)
        value = jnp.concatenate([before, value, after], axis=dim)
    return value


def with_halo_many(values, sides, width):
    values = list(values)
    for place, axis in enumerate(("gx", "gy")):
        size = lax.axis_size(axis)
        up = [(i, (i + 1) % size) for i in range(size - 1)]
        down = [(j, i) for i, j in up]
        lasts, initials = [], []
        for value, dims in zip(values, sides):
            dim = dims[place]
            length = value.shape[dim]
            lasts.append(lax.slice_in_dim(value, length - width, length, axis=dim))
            initials.append(lax.slice_in_dim(value, 0, width, axis=dim))
        before_all = lax.ppermute(jnp.concatenate([p.reshape(-1) for p in lasts]), axis, up)
        after_all = lax.ppermute(jnp.concatenate([p.reshape(-1) for p in initials]), axis, down)
        offset = 0
        for index, (value, dims) in enumerate(zip(values, sides)):
            shape = lasts[index].shape
            count = lasts[index].size
            before = before_all[offset : offset + count].reshape(shape)
            after = after_all[offset : offset + count].reshape(shape)
            offset += count
            values[index] = jnp.concatenate([before, value, after], axis=dims[place])
    return values


def butterfly_sum(value, axes):
    for axis in axes:
        size = lax.axis_size(axis)
        stride = 1
        while stride < size:
            partners = [(i, i ^ stride) for i in range(size)]
            value = value + lax.ppermute(value, axis, partners)
            stride *= 2
    return value


def apply_stencil(window, stiff_block):
    paddings = [(0, 0)] * (window.ndim - 1) + [(1, 1)]
    widened = jnp.pad(window, paddings)
    along_first = widened[..., :-2, :, :] + widened[..., 1:-1, :, :] + widened[..., 2:, :, :]
    along_second = (
        along_first[..., :, :-2, :] + along_first[..., :, 1:-1, :] + along_first[..., :, 2:, :]
    )
    box_sum = along_second[..., :-2] + along_second[..., 1:-1] + along_second[..., 2:]
    centre = window[..., 1:-1, 1:-1, :]
    slope_first = widened[..., 2:, :, :] - widened[..., :-2, :, :]
    slope_second = widened[..., 1:-1, 2:, :] - widened[..., 1:-1, :-2, :]
    mixed_ab = slope_first[..., :, 2:, 1:-1] - slope_first[..., :, :-2, 1:-1]
    mixed_ac = slope_first[..., :, 1:-1, 2:] - slope_first[..., :, 1:-1, :-2]
    mixed_bc = slope_second[..., 2:] - slope_second[..., :-2]
    cross_terms = jnp.stack(
        [
            mixed_ab[..., 1, :, :, :] + mixed_ac[..., 2, :, :, :],
            mixed_ab[..., 0, :, :, :] + mixed_bc[..., 2, :, :, :],
            mixed_ac[..., 0, :, :, :] + mixed_bc[..., 1, :, :, :],
        ],
        axis=-4,
    )
    return (27.0 + stiff_block) * centre - box_sum + mixing * cross_terms


def window_plan(offset, length):
    if offset == 0:
        return (0, length + 2, 1, length + 1, 0, length)
    if offset == 1:
        return (length - 1, length + 2, 2, 3, length - 1, length)
    return (0, 3, 0, 1, 0, 1)


def select_mask(plan):
    places = jnp.arange(plan[1] - plan[0])
    return ((places >= plan[2]) & (places < plan[3])).astype(jnp.float32)


def coarse_tile(padded, own_panels, stiff_block, shift_first, shift_second):
    plan_first = window_plan(shift_first, own_panels.shape[2])
    plan_second = window_plan(shift_second, own_panels.shape[3])
    window = padded[:, :, plan_first[0] : plan_first[1], plan_second[0] : plan_second[1], :]
    keep_first = select_mask(plan_first)
    keep_second = select_mask(plan_second)
    masked = window * (keep_first[:, None, None] * keep_second[None, :, None])
    imaged = apply_stencil(
        masked, stiff_block[plan_first[4] : plan_first[5], plan_second[4] : plan_second[5], :]
    )
    panel_part = own_panels[:, :, plan_first[4] : plan_first[5], plan_second[4] : plan_second[5], :]
    return jnp.einsum("kabcd,labcd->kl", panel_part, imaged, precision=precise)


def jacobi(ext_residual, ext_stiff):
    inv_diag = damping / (26.0 + ext_stiff)
    correction = inv_diag * ext_residual
    for sweep_index in range(SWEEPS - 1):
        widened = jnp.pad(correction, ((0, 0), (1, 1), (1, 1), (0, 0)))
        correction = correction + inv_diag * (ext_residual - apply_stencil(widened, ext_stiff))
    return correction


def fold_axis(spread, dimension, length):
    interior = lax.slice_in_dim(spread, 2, 2 + length, axis=dimension)
    lower_part = lax.slice_in_dim(spread, 0, 1, axis=dimension)
    upper_part = lax.slice_in_dim(spread, length + 3, length + 4, axis=dimension)
    pads_low = [(0, 0)] * spread.ndim
    pads_high = [(0, 0)] * spread.ndim
    pads_low[dimension] = (0, length - 1)
    pads_high[dimension] = (length - 1, 0)
    return interior + jnp.pad(lower_part, pads_low) + jnp.pad(upper_part, pads_high)


def per_device(right_side, stiffness, panels):
    cells_first = stiffness.shape[0]
    cells_second = stiffness.shape[1]
    padded, ext_stiff, ext_right = with_halo_many(
        (panels, stiffness, right_side), ((2, 3), (0, 1), (1, 2)), 1
    )
    diag_tile = coarse_tile(padded, panels, stiffness, 0, 0)
    tile_list = [
        coarse_tile(padded, panels, stiffness, shift_first, shift_second)
        for shift_first, shift_second in neighbours
    ]
    weights = damping / jnp.diagonal(diag_tile)

    def precondition(current, ext_residual=None):
        restricted = jnp.einsum("kabcd,abcd->k", panels, current, precision=precise)
        first_guess = weights * restricted
        if ext_residual is None:
            nearby, ext_residual = with_halo_many(
                (first_guess[None, None], current), ((0, 1), (1, 2)), 1
            )
        else:
            (nearby,) = with_halo_many((first_guess[None, None],), ((0, 1),), 1)
        applied = jnp.dot(diag_tile, first_guess, precision=precise)
        for place, (shift_first, shift_second) in enumerate(neighbours):
            applied = applied + jnp.dot(
                tile_list[place], nearby[1 + shift_first, 1 + shift_second], precision=precise
            )
        coarse_vec = first_guess + weights * (restricted - applied)
        coarse_part = jnp.einsum("k,kabcd->abcd", coarse_vec, panels, precision=precise)
        correction = jacobi(ext_residual, ext_stiff)
        spread = with_halo(correction, (("gx", 1), ("gy", 2)), 1)
        folded = fold_axis(fold_axis(spread, 1, cells_first), 2, cells_second)
        return folded + coarse_part

    def operate(field):
        return apply_stencil(with_halo(field, (("gx", 1), ("gy", 2)), 1), stiffness)

    residual = right_side
    precond = precondition(residual, ext_right)
    imaged = operate(precond)
    smoothed = precondition(imaged)
    twice = operate(smoothed)
    local_dots = jnp.stack(
        [
            jnp.sum(residual * precond),
            jnp.sum(precond * imaged),
            jnp.sum(residual * smoothed),
            jnp.sum(imaged * smoothed),
            jnp.sum(precond * twice),
            jnp.sum(smoothed * twice),
        ]
    )
    fit, curve, cross_r, cross_q, cross_z, curve_w = butterfly_sum(local_dots, ("gx", "gy"))
    step_first = fit / curve
    solution = step_first * precond
    residual = residual - step_first * imaged
    fit_next = fit - step_first * (curve + cross_r) + step_first * step_first * cross_q
    ratio = fit_next / fit
    grown = 1.0 + ratio
    curve_next = (
        grown * grown * curve
        - step_first * grown * (cross_z + cross_q)
        + step_first * step_first * curve_w
    )
    step_second = fit_next / curve_next
    precond_next = precond - step_first * smoothed
    direction = precond_next + ratio * precond
    imaged_next = (imaged - step_first * twice) + ratio * imaged
    solution = solution + step_second * direction
    residual = residual - step_second * imaged_next
    coupling = jnp.stack(tile_list).reshape(1, 1, 8, -1)
    return (solution, residual, coupling)


def solution(mesh):
    return jax.shard_map(
        per_device,
        mesh=mesh,
        in_specs=(P(None, "gx", "gy", None), P("gx", "gy", None), P(None, None, "gx", "gy", None)),
        out_specs=(P(None, "gx", "gy", None), P(None, "gx", "gy", None), P("gx", "gy", None, None)),
        check_vma=False,
    )
```

```python
import jax
import jax.numpy as jnp
from jax import lax
from jax.sharding import PartitionSpec as P

SWEEPS = 4
ITERS = 2


precise = lax.Precision.HIGHEST
mixing = 0.25
damping = 0.5
neighbours = ((-1, -1), (-1, 0), (-1, 1), (0, -1), (0, 1), (1, -1), (1, 0), (1, 1))


def with_halo(value, sides, width):
    for axis, dim in sides:
        size, length = (lax.axis_size(axis), value.shape[dim])
        up = [(i, (i + 1) % size) for i in range(size - 1)]
        down = [(j, i) for i, j in up]
        last = lax.slice_in_dim(value, length - width, length, axis=dim)
        initial = lax.slice_in_dim(value, 0, width, axis=dim)
        before = lax.ppermute(last, axis, up)
        after = lax.ppermute(initial, axis, down)
        value = jnp.concatenate([before, value, after], axis=dim)
    return value


def butterfly_sum(value, axes):
    for axis in axes:
        size = lax.axis_size(axis)
        stride = 1
        while stride < size:
            partners = [(i, i ^ stride) for i in range(size)]
            value = value + lax.ppermute(value, axis, partners)
            stride *= 2
    return value


def apply_stencil(window, stiff_block):
    paddings = [(0, 0)] * (window.ndim - 1) + [(1, 1)]
    widened = jnp.pad(window, paddings)
    along_first = widened[..., :-2, :, :] + widened[..., 1:-1, :, :] + widened[..., 2:, :, :]
    along_second = (
        along_first[..., :, :-2, :] + along_first[..., :, 1:-1, :] + along_first[..., :, 2:, :]
    )
    box_sum = along_second[..., :-2] + along_second[..., 1:-1] + along_second[..., 2:]
    centre = window[..., 1:-1, 1:-1, :]
    slope_first = widened[..., 2:, :, :] - widened[..., :-2, :, :]
    slope_second = widened[..., 1:-1, 2:, :] - widened[..., 1:-1, :-2, :]
    mixed_ab = slope_first[..., :, 2:, 1:-1] - slope_first[..., :, :-2, 1:-1]
    mixed_ac = slope_first[..., :, 1:-1, 2:] - slope_first[..., :, 1:-1, :-2]
    mixed_bc = slope_second[..., 2:] - slope_second[..., :-2]
    cross_terms = jnp.stack(
        [
            mixed_ab[..., 1, :, :, :] + mixed_ac[..., 2, :, :, :],
            mixed_ab[..., 0, :, :, :] + mixed_bc[..., 2, :, :, :],
            mixed_ac[..., 0, :, :, :] + mixed_bc[..., 1, :, :, :],
        ],
        axis=-4,
    )
    return (27.0 + stiff_block) * centre - box_sum + mixing * cross_terms


def window_plan(offset, length):
    if offset == 0:
        return (0, length + 2, 1, length + 1, 0, length)
    if offset == 1:
        return (length - 1, length + 2, 2, 3, length - 1, length)
    return (0, 3, 0, 1, 0, 1)


def select_mask(plan):
    places = jnp.arange(plan[1] - plan[0])
    return ((places >= plan[2]) & (places < plan[3])).astype(jnp.float32)


def coarse_tile(padded, own_panels, stiff_block, shift_first, shift_second):
    plan_first = window_plan(shift_first, own_panels.shape[2])
    plan_second = window_plan(shift_second, own_panels.shape[3])
    window = padded[:, :, plan_first[0] : plan_first[1], plan_second[0] : plan_second[1], :]
    keep_first = select_mask(plan_first)
    keep_second = select_mask(plan_second)
    masked = window * (keep_first[:, None, None] * keep_second[None, :, None])
    imaged = apply_stencil(
        masked, stiff_block[plan_first[4] : plan_first[5], plan_second[4] : plan_second[5], :]
    )
    panel_part = own_panels[:, :, plan_first[4] : plan_first[5], plan_second[4] : plan_second[5], :]
    return jnp.einsum("kabcd,labcd->kl", panel_part, imaged, precision=precise)


def jacobi(ext_residual, ext_stiff):
    inv_diag = damping / (26.0 + ext_stiff)
    correction = inv_diag * ext_residual
    for sweep_index in range(SWEEPS - 1):
        widened = jnp.pad(correction, ((0, 0), (1, 1), (1, 1), (0, 0)))
        correction = correction + inv_diag * (ext_residual - apply_stencil(widened, ext_stiff))
    return correction


def fold_axis(spread, dimension, length):
    interior = lax.slice_in_dim(spread, 2, 2 + length, axis=dimension)
    lower_part = lax.slice_in_dim(spread, 0, 1, axis=dimension)
    upper_part = lax.slice_in_dim(spread, length + 3, length + 4, axis=dimension)
    pads_low = [(0, 0)] * spread.ndim
    pads_high = [(0, 0)] * spread.ndim
    pads_low[dimension] = (0, length - 1)
    pads_high[dimension] = (length - 1, 0)
    return interior + jnp.pad(lower_part, pads_low) + jnp.pad(upper_part, pads_high)


def per_device(right_side, stiffness, panels):
    cells_first = stiffness.shape[0]
    cells_second = stiffness.shape[1]
    padded, stiff_wide = (
        with_halo(panels, (("gx", 2), ("gy", 3)), 1),
        with_halo(stiffness[None, None], (("gx", 2), ("gy", 3)), 1),
    )
    ext_stiff = stiff_wide[0, 0]
    own_wide = jnp.pad(panels, ((0, 0), (0, 0), (1, 1), (1, 1), (0, 0)))
    diag_tile = coarse_tile(own_wide, panels, stiffness, 0, 0)
    tile_list = [
        coarse_tile(padded, panels, stiffness, shift_first, shift_second)
        for shift_first, shift_second in neighbours
    ]
    weights = damping / jnp.diagonal(diag_tile)

    def precondition(current):
        restricted = jnp.einsum("kabcd,abcd->k", panels, current, precision=precise)
        first_guess = weights * restricted
        nearby = with_halo(first_guess[None, None], (("gx", 0), ("gy", 1)), 1)
        applied = jnp.dot(diag_tile, first_guess, precision=precise)
        for place, (shift_first, shift_second) in enumerate(neighbours):
            applied = applied + jnp.dot(
                tile_list[place], nearby[1 + shift_first, 1 + shift_second], precision=precise
            )
        coarse_vec = first_guess + weights * (restricted - applied)
        coarse_part = jnp.einsum("k,kabcd->abcd", coarse_vec, panels, precision=precise)
        ext_residual = with_halo(current, (("gx", 1), ("gy", 2)), 1)
        correction = jacobi(ext_residual, ext_stiff)
        spread = with_halo(correction, (("gx", 1), ("gy", 2)), 1)
        folded = fold_axis(fold_axis(spread, 1, cells_first), 2, cells_second)
        return folded + coarse_part

    def operate(field):
        return apply_stencil(with_halo(field, (("gx", 1), ("gy", 2)), 1), stiffness)

    residual = right_side
    precond = precondition(residual)
    imaged = operate(precond)
    smoothed = precondition(imaged)
    twice = operate(smoothed)
    local_dots = jnp.stack(
        [
            jnp.sum(residual * precond),
            jnp.sum(precond * imaged),
            jnp.sum(residual * smoothed),
            jnp.sum(imaged * smoothed),
            jnp.sum(precond * twice),
            jnp.sum(smoothed * twice),
        ]
    )
    fit, curve, cross_r, cross_q, cross_z, curve_w = butterfly_sum(local_dots, ("gx", "gy"))
    step_first = fit / curve
    solution = step_first * precond
    residual = residual - step_first * imaged
    fit_next = fit - step_first * (curve + cross_r) + step_first * step_first * cross_q
    ratio = fit_next / fit
    grown = 1.0 + ratio
    curve_next = (
        grown * grown * curve
        - step_first * grown * (cross_z + cross_q)
        + step_first * step_first * curve_w
    )
    step_second = fit_next / curve_next
    precond_next = precond - step_first * smoothed
    direction = precond_next + ratio * precond
    imaged_next = (imaged - step_first * twice) + ratio * imaged
    solution = solution + step_second * direction
    residual = residual - step_second * imaged_next
    coupling = jnp.stack(tile_list).reshape(1, 1, 8, -1)
    return (solution, residual, coupling)


def solution(mesh):
    return jax.shard_map(
        per_device,
        mesh=mesh,
        in_specs=(P(None, "gx", "gy", None), P("gx", "gy", None), P(None, None, "gx", "gy", None)),
        out_specs=(P(None, "gx", "gy", None), P(None, "gx", "gy", None), P("gx", "gy", None, None)),
        check_vma=False,
    )
```

```python
import jax
import jax.numpy as jnp
from jax import lax
from jax.sharding import PartitionSpec as P

SWEEPS = 4
ITERS = 2


precise = lax.Precision.HIGHEST
mixing = 0.25
damping = 0.5
neighbours = ((-1, -1), (-1, 0), (-1, 1), (0, -1), (0, 1), (1, -1), (1, 0), (1, 1))


def with_halo(value, sides, width):
    for axis, dim in sides:
        size, length = (lax.axis_size(axis), value.shape[dim])
        up = [(i, (i + 1) % size) for i in range(size - 1)]
        down = [(j, i) for i, j in up]
        last = lax.slice_in_dim(value, length - width, length, axis=dim)
        initial = lax.slice_in_dim(value, 0, width, axis=dim)
        before = lax.ppermute(last, axis, up)
        after = lax.ppermute(initial, axis, down)
        value = jnp.concatenate([before, value, after], axis=dim)
    return value


def butterfly_sum(value, axes):
    for axis in axes:
        size = lax.axis_size(axis)
        stride = 1
        while stride < size:
            partners = [(i, i ^ stride) for i in range(size)]
            value = value + lax.ppermute(value, axis, partners)
            stride *= 2
    return value


def apply_stencil(window, stiff_block):
    paddings = [(0, 0)] * (window.ndim - 1) + [(1, 1)]
    widened = jnp.pad(window, paddings)
    along_first = widened[..., :-2, :, :] + widened[..., 1:-1, :, :] + widened[..., 2:, :, :]
    along_second = (
        along_first[..., :, :-2, :] + along_first[..., :, 1:-1, :] + along_first[..., :, 2:, :]
    )
    box_sum = along_second[..., :-2] + along_second[..., 1:-1] + along_second[..., 2:]
    centre = window[..., 1:-1, 1:-1, :]
    slope_first = widened[..., 2:, :, :] - widened[..., :-2, :, :]
    slope_second = widened[..., 1:-1, 2:, :] - widened[..., 1:-1, :-2, :]
    mixed_ab = slope_first[..., :, 2:, 1:-1] - slope_first[..., :, :-2, 1:-1]
    mixed_ac = slope_first[..., :, 1:-1, 2:] - slope_first[..., :, 1:-1, :-2]
    mixed_bc = slope_second[..., 2:] - slope_second[..., :-2]
    cross_terms = jnp.stack(
        [
            mixed_ab[..., 1, :, :, :] + mixed_ac[..., 2, :, :, :],
            mixed_ab[..., 0, :, :, :] + mixed_bc[..., 2, :, :, :],
            mixed_ac[..., 0, :, :, :] + mixed_bc[..., 1, :, :, :],
        ],
        axis=-4,
    )
    return (27.0 + stiff_block) * centre - box_sum + mixing * cross_terms


def window_plan(offset, length):
    if offset == 0:
        return (0, length + 2, 1, length + 1, 0, length)
    if offset == 1:
        return (length - 1, length + 2, 2, 3, length - 1, length)
    return (0, 3, 0, 1, 0, 1)


def select_mask(plan):
    places = jnp.arange(plan[1] - plan[0])
    return ((places >= plan[2]) & (places < plan[3])).astype(jnp.float32)


def coarse_tile(padded, own_panels, stiff_block, shift_first, shift_second):
    plan_first = window_plan(shift_first, own_panels.shape[2])
    plan_second = window_plan(shift_second, own_panels.shape[3])
    window = padded[:, :, plan_first[0] : plan_first[1], plan_second[0] : plan_second[1], :]
    keep_first = select_mask(plan_first)
    keep_second = select_mask(plan_second)
    masked = window * (keep_first[:, None, None] * keep_second[None, :, None])
    imaged = apply_stencil(
        masked, stiff_block[plan_first[4] : plan_first[5], plan_second[4] : plan_second[5], :]
    )
    panel_part = own_panels[:, :, plan_first[4] : plan_first[5], plan_second[4] : plan_second[5], :]
    return jnp.einsum("kabcd,labcd->kl", panel_part, imaged, precision=precise)


def jacobi(ext_residual, ext_stiff):
    inv_diag = damping / (26.0 + ext_stiff)
    correction = inv_diag * ext_residual
    for sweep_index in range(SWEEPS - 1):
        widened = jnp.pad(correction, ((0, 0), (1, 1), (1, 1), (0, 0)))
        correction = correction + inv_diag * (ext_residual - apply_stencil(widened, ext_stiff))
    return correction


def inside_grid(cells_first, cells_second):
    keep = []
    for axis, length in (("gx", cells_first), ("gy", cells_second)):
        index, size = lax.axis_index(axis), lax.axis_size(axis)
        places = jnp.arange(length + 2)
        low = jnp.where(index == 0, 1, 0)
        high = jnp.where(index == size - 1, length, length + 1)
        keep.append(((places >= low) & (places <= high)).astype(jnp.float32))
    return keep[0][:, None, None] * keep[1][None, :, None]


def fold_axis(spread, dimension, length):
    interior = lax.slice_in_dim(spread, 2, 2 + length, axis=dimension)
    lower_part = lax.slice_in_dim(spread, 0, 1, axis=dimension)
    upper_part = lax.slice_in_dim(spread, length + 3, length + 4, axis=dimension)
    pads_low = [(0, 0)] * spread.ndim
    pads_high = [(0, 0)] * spread.ndim
    pads_low[dimension] = (0, length - 1)
    pads_high[dimension] = (length - 1, 0)
    return interior + jnp.pad(lower_part, pads_low) + jnp.pad(upper_part, pads_high)


def per_device(right_side, stiffness, panels):
    cells_first = stiffness.shape[0]
    cells_second = stiffness.shape[1]
    padded, stiff_wide = (
        with_halo(panels, (("gx", 2), ("gy", 3)), 1),
        with_halo(stiffness[None, None], (("gx", 2), ("gy", 3)), 1),
    )
    ext_stiff = stiff_wide[0, 0]
    own_wide = jnp.pad(panels, ((0, 0), (0, 0), (1, 1), (1, 1), (0, 0)))
    diag_tile = coarse_tile(own_wide, panels, stiffness, 0, 0)
    tile_list = [
        coarse_tile(padded, panels, stiffness, shift_first, shift_second)
        for shift_first, shift_second in neighbours
    ]
    weights = damping / jnp.diagonal(diag_tile)

    def precondition(current, ext_residual=None):
        restricted = jnp.einsum("kabcd,abcd->k", panels, current, precision=precise)
        first_guess = weights * restricted
        nearby = with_halo(first_guess[None, None], (("gx", 0), ("gy", 1)), 1)
        applied = jnp.dot(diag_tile, first_guess, precision=precise)
        for place, (shift_first, shift_second) in enumerate(neighbours):
            applied = applied + jnp.dot(
                tile_list[place], nearby[1 + shift_first, 1 + shift_second], precision=precise
            )
        coarse_vec = first_guess + weights * (restricted - applied)
        coarse_part = jnp.einsum("k,kabcd->abcd", coarse_vec, panels, precision=precise)
        if ext_residual is None:
            ext_residual = with_halo(current, (("gx", 1), ("gy", 2)), 1)
        correction = jacobi(ext_residual, ext_stiff)
        spread = with_halo(correction, (("gx", 1), ("gy", 2)), 1)
        folded = fold_axis(fold_axis(spread, 1, cells_first), 2, cells_second)
        return folded + coarse_part

    def operate(field):
        return apply_stencil(with_halo(field, (("gx", 1), ("gy", 2)), 1), stiffness)

    residual = right_side
    precond = precondition(residual)
    ext_imaged = apply_stencil(with_halo(precond, (("gx", 1), ("gy", 2)), 2), ext_stiff)
    ext_imaged = ext_imaged * inside_grid(cells_first, cells_second)
    imaged = ext_imaged[:, 1:-1, 1:-1, :]
    smoothed = precondition(imaged, ext_imaged)
    twice = operate(smoothed)
    local_dots = jnp.stack(
        [
            jnp.sum(residual * precond),
            jnp.sum(precond * imaged),
            jnp.sum(residual * smoothed),
            jnp.sum(imaged * smoothed),
            jnp.sum(precond * twice),
            jnp.sum(smoothed * twice),
        ]
    )
    fit, curve, cross_r, cross_q, cross_z, curve_w = butterfly_sum(local_dots, ("gx", "gy"))
    step_first = fit / curve
    solution = step_first * precond
    residual = residual - step_first * imaged
    fit_next = fit - step_first * (curve + cross_r) + step_first * step_first * cross_q
    ratio = fit_next / fit
    grown = 1.0 + ratio
    curve_next = (
        grown * grown * curve
        - step_first * grown * (cross_z + cross_q)
        + step_first * step_first * curve_w
    )
    step_second = fit_next / curve_next
    precond_next = precond - step_first * smoothed
    direction = precond_next + ratio * precond
    imaged_next = (imaged - step_first * twice) + ratio * imaged
    solution = solution + step_second * direction
    residual = residual - step_second * imaged_next
    coupling = jnp.stack(tile_list).reshape(1, 1, 8, -1)
    return (solution, residual, coupling)


def solution(mesh):
    return jax.shard_map(
        per_device,
        mesh=mesh,
        in_specs=(P(None, "gx", "gy", None), P("gx", "gy", None), P(None, None, "gx", "gy", None)),
        out_specs=(P(None, "gx", "gy", None), P(None, "gx", "gy", None), P("gx", "gy", None, None)),
        check_vma=False,
    )
```

```python
import jax
import jax.numpy as jnp
from jax import lax
from jax.sharding import PartitionSpec as P

SWEEPS = 4


precise = lax.Precision.HIGHEST
mixing = 0.25
damping = 0.5
neighbours = ((-1, -1), (-1, 0), (-1, 1), (0, -1), (0, 1), (1, -1), (1, 0), (1, 1))


def with_halo(value, sides, width):
    for axis, dim in sides:
      size, length = (lax.axis_size(axis), value.shape[dim])
      up = [(i, (i + 1) % size) for i in range(size - 1)]
      down = [(j, i) for i, j in up]
      last = lax.slice_in_dim(value, length - width, length, axis=dim)
      initial = lax.slice_in_dim(value, 0, width, axis=dim)
      before = lax.ppermute(last, axis, up)
      after = lax.ppermute(initial, axis, down)
      value = jnp.concatenate([before, value, after], axis=dim)
    return value


def butterfly_sum(value, axes):
    for axis in axes:
        size = lax.axis_size(axis)
        stride = 1
        while stride < size:
            partners = [(i, i ^ stride) for i in range(size)]
            value = value + lax.ppermute(value, axis, partners)
            stride *= 2
    return value


def apply_stencil(window, stiff_block):
    paddings = [(0, 0)] * (window.ndim - 1) + [(1, 1)]
    widened = jnp.pad(window, paddings)
    along_first = widened[..., :-2, :, :] + widened[..., 1:-1, :, :] + widened[..., 2:, :, :]
    along_second = (
        along_first[..., :, :-2, :] + along_first[..., :, 1:-1, :] + along_first[..., :, 2:, :]
    )
    box_sum = along_second[..., :-2] + along_second[..., 1:-1] + along_second[..., 2:]
    centre = window[..., 1:-1, 1:-1, :]
    slope_first = widened[..., 2:, :, :] - widened[..., :-2, :, :]
    slope_second = widened[..., 1:-1, 2:, :] - widened[..., 1:-1, :-2, :]
    mixed_ab = slope_first[..., :, 2:, 1:-1] - slope_first[..., :, :-2, 1:-1]
    mixed_ac = slope_first[..., :, 1:-1, 2:] - slope_first[..., :, 1:-1, :-2]
    mixed_bc = slope_second[..., 2:] - slope_second[..., :-2]
    cross_terms = jnp.stack(
        [
            mixed_ab[..., 1, :, :, :] + mixed_ac[..., 2, :, :, :],
            mixed_ab[..., 0, :, :, :] + mixed_bc[..., 2, :, :, :],
            mixed_ac[..., 0, :, :, :] + mixed_bc[..., 1, :, :, :],
        ],
        axis=-4,
    )
    return (27.0 + stiff_block) * centre - box_sum + mixing * cross_terms


def window_plan(offset, length):
    if offset == 0:
        return (0, length + 2, 1, length + 1, 0, length)
    if offset == 1:
        return (length - 1, length + 2, 2, 3, length - 1, length)
    return (0, 3, 0, 1, 0, 1)


def select_mask(plan):
    places = jnp.arange(plan[1] - plan[0])
    return ((places >= plan[2]) & (places < plan[3])).astype(jnp.float32)


def coarse_tile(padded, own_panels, stiff_block, shift_first, shift_second):
    plan_first = window_plan(shift_first, own_panels.shape[2])
    plan_second = window_plan(shift_second, own_panels.shape[3])
    window = padded[:, :, plan_first[0] : plan_first[1], plan_second[0] : plan_second[1], :]
    keep_first = select_mask(plan_first)
    keep_second = select_mask(plan_second)
    masked = window * (keep_first[:, None, None] * keep_second[None, :, None])
    imaged = apply_stencil(
        masked, stiff_block[plan_first[4] : plan_first[5], plan_second[4] : plan_second[5], :]
    )
    panel_part = own_panels[:, :, plan_first[4] : plan_first[5], plan_second[4] : plan_second[5], :]
    return jnp.einsum("kabcd,labcd->kl", panel_part, imaged, precision=precise)


def jacobi(ext_residual, ext_stiff):
    inv_diag = damping / (26.0 + ext_stiff)
    correction = inv_diag * ext_residual
    for _ in range(SWEEPS - 1):
        widened = jnp.pad(correction, ((0, 0), (1, 1), (1, 1), (0, 0)))
        correction = correction + inv_diag * (ext_residual - apply_stencil(widened, ext_stiff))
    return correction


def inside_grid(cells_first, cells_second):
    keep = []
    for axis, length in (("gx", cells_first), ("gy", cells_second)):
        index, size = lax.axis_index(axis), lax.axis_size(axis)
        places = jnp.arange(length + 2)
        low = jnp.where(index == 0, 1, 0)
        high = jnp.where(index == size - 1, length, length + 1)
        keep.append(((places >= low) & (places <= high)).astype(jnp.float32))
    return keep[0][:, None, None] * keep[1][None, :, None]


def fold_axis(spread, dimension, length):
    interior = lax.slice_in_dim(spread, 2, 2 + length, axis=dimension)
    lower_part = lax.slice_in_dim(spread, 0, 1, axis=dimension)
    upper_part = lax.slice_in_dim(spread, length + 3, length + 4, axis=dimension)
    pads_low = [(0, 0)] * spread.ndim
    pads_high = [(0, 0)] * spread.ndim
    pads_low[dimension] = (0, length - 1)
    pads_high[dimension] = (length - 1, 0)
    return interior + jnp.pad(lower_part, pads_low) + jnp.pad(upper_part, pads_high)


def per_device_body(right_side, stiffness, panels):
    cells_first = stiffness.shape[0]
    cells_second = stiffness.shape[1]
    padded, stiff_wide = (
        with_halo(panels, (("gx", 2), ("gy", 3)), 1),
        with_halo(stiffness[None, None], (("gx", 2), ("gy", 3)), 1),
    )
    ext_stiff = stiff_wide[0, 0]
    own_wide = jnp.pad(panels, ((0, 0), (0, 0), (1, 1), (1, 1), (0, 0)))
    diag_tile = coarse_tile(own_wide, panels, stiffness, 0, 0)
    tile_list = [
        coarse_tile(padded, panels, stiffness, shift_first, shift_second)
        for shift_first, shift_second in neighbours
    ]
    weights = damping / jnp.diagonal(diag_tile)

    def precondition(current, ext_residual=None):
        restricted = jnp.einsum("kabcd,abcd->k", panels, current, precision=precise)
        first_guess = weights * restricted
        nearby = with_halo(first_guess[None, None], (("gx", 0), ("gy", 1)), 1)
        applied = jnp.dot(diag_tile, first_guess, precision=precise)
        for place, (shift_first, shift_second) in enumerate(neighbours):
            applied = applied + jnp.dot(
                tile_list[place], nearby[1 + shift_first, 1 + shift_second], precision=precise
            )
        coarse_vec = first_guess + weights * (restricted - applied)
        coarse_part = jnp.einsum("k,kabcd->abcd", coarse_vec, panels, precision=precise)
        if ext_residual is None:
            ext_residual = with_halo(current, (("gx", 1), ("gy", 2)), 1)
        correction = jacobi(ext_residual, ext_stiff)
        spread = with_halo(correction, (("gx", 1), ("gy", 2)), 1)
        folded = fold_axis(fold_axis(spread, 1, cells_first), 2, cells_second)
        return folded + coarse_part

    def operate(field):
        return apply_stencil(with_halo(field, (("gx", 1), ("gy", 2)), 1), stiffness)

    residual = right_side
    precond = precondition(residual)
    ext_imaged = apply_stencil(with_halo(precond, (("gx", 1), ("gy", 2)), 2), ext_stiff)
    ext_imaged = ext_imaged * inside_grid(cells_first, cells_second)
    imaged = ext_imaged[:, 1:-1, 1:-1, :]
    smoothed = precondition(imaged, ext_imaged)
    twice = operate(smoothed)
    local_dots = jnp.stack(
        [
            jnp.sum(residual * precond),
            jnp.sum(precond * imaged),
            jnp.sum(residual * smoothed),
            jnp.sum(imaged * smoothed),
            jnp.sum(precond * twice),
            jnp.sum(smoothed * twice),
        ]
    )
    fit, curve, cross_r, cross_q, cross_z, curve_w = butterfly_sum(local_dots, ("gx", "gy"))
    step_first = fit / curve
    solution = step_first * precond
    residual = residual - step_first * imaged
    fit_next = fit - step_first * (curve + cross_r) + step_first * step_first * cross_q
    ratio = fit_next / fit
    grown = 1.0 + ratio
    curve_next = (
        grown * grown * curve
        - step_first * grown * (cross_z + cross_q)
        + step_first * step_first * curve_w
    )
    step_second = fit_next / curve_next
    precond_next = precond - step_first * smoothed
    direction = precond_next + ratio * precond
    imaged_next = (imaged - step_first * twice) + ratio * imaged
    solution = solution + step_second * direction
    residual = residual - step_second * imaged_next
    coupling = jnp.stack(tile_list).reshape(1, 1, 8, -1)
    return (solution, residual, coupling)


def solution(mesh):
    return jax.shard_map(
        per_device_body,
        mesh=mesh,
        in_specs=(P(None, "gx", "gy", None), P("gx", "gy", None), P(None, None, "gx", "gy", None)),
        out_specs=(P(None, "gx", "gy", None), P(None, "gx", "gy", None), P("gx", "gy", None, None)),
        check_vma=False,
    )
```

```python
import jax
import jax.numpy as jnp
from jax import lax
from jax.sharding import PartitionSpec as P

SWEEPS = 4


precise = lax.Precision.HIGHEST
mixing = 0.25
damping = 0.5
neighbours = ((-1, -1), (-1, 0), (-1, 1), (0, -1), (0, 1), (1, -1), (1, 0), (1, 1))


def with_halo(value, sides, width):
    for axis, dim in sides:
      size, length = (lax.axis_size(axis), value.shape[dim])
      up = [(i, (i + 1) % size) for i in range(size - 1)]
      down = [(j, i) for i, j in up]
      last = lax.slice_in_dim(value, length - width, length, axis=dim)
      initial = lax.slice_in_dim(value, 0, width, axis=dim)
      before = lax.ppermute(last, axis, up)
      after = lax.ppermute(initial, axis, down)
      value = jnp.concatenate([before, value, after], axis=dim)
    return value


def with_halo_stacked(arrays, width):
    arrays = list(arrays)
    for axis, dim in (("gx", 2), ("gy", 3)):
        size, length = lax.axis_size(axis), arrays[0].shape[dim]
        up = [(i, (i + 1) % size) for i in range(size - 1)]
        down = [(j, i) for i, j in up]
        lasts = [lax.slice_in_dim(a, length - width, length, axis=dim) for a in arrays]
        initials = [lax.slice_in_dim(a, 0, width, axis=dim) for a in arrays]
        before_all = lax.ppermute(jnp.concatenate(lasts, axis=0), axis, up)
        after_all = lax.ppermute(jnp.concatenate(initials, axis=0), axis, down)
        offset = 0
        for index, a in enumerate(arrays):
            count = a.shape[0]
            before = before_all[offset : offset + count]
            after = after_all[offset : offset + count]
            offset += count
            arrays[index] = jnp.concatenate([before, a, after], axis=dim)
    return arrays


def butterfly_sum(value, axes):
    for axis in axes:
        size = lax.axis_size(axis)
        stride = 1
        while stride < size:
            partners = [(i, i ^ stride) for i in range(size)]
            value = value + lax.ppermute(value, axis, partners)
            stride *= 2
    return value


def apply_stencil(window, stiff_block):
    paddings = [(0, 0)] * (window.ndim - 1) + [(1, 1)]
    widened = jnp.pad(window, paddings)
    along_first = widened[..., :-2, :, :] + widened[..., 1:-1, :, :] + widened[..., 2:, :, :]
    along_second = (
        along_first[..., :, :-2, :] + along_first[..., :, 1:-1, :] + along_first[..., :, 2:, :]
    )
    box_sum = along_second[..., :-2] + along_second[..., 1:-1] + along_second[..., 2:]
    centre = window[..., 1:-1, 1:-1, :]
    slope_first = widened[..., 2:, :, :] - widened[..., :-2, :, :]
    slope_second = widened[..., 1:-1, 2:, :] - widened[..., 1:-1, :-2, :]
    mixed_ab = slope_first[..., :, 2:, 1:-1] - slope_first[..., :, :-2, 1:-1]
    mixed_ac = slope_first[..., :, 1:-1, 2:] - slope_first[..., :, 1:-1, :-2]
    mixed_bc = slope_second[..., 2:] - slope_second[..., :-2]
    cross_terms = jnp.stack(
        [
            mixed_ab[..., 1, :, :, :] + mixed_ac[..., 2, :, :, :],
            mixed_ab[..., 0, :, :, :] + mixed_bc[..., 2, :, :, :],
            mixed_ac[..., 0, :, :, :] + mixed_bc[..., 1, :, :, :],
        ],
        axis=-4,
    )
    return (27.0 + stiff_block) * centre - box_sum + mixing * cross_terms


def window_plan(offset, length):
    if offset == 0:
        return (0, length + 2, 1, length + 1, 0, length)
    if offset == 1:
        return (length - 1, length + 2, 2, 3, length - 1, length)
    return (0, 3, 0, 1, 0, 1)


def select_mask(plan):
    places = jnp.arange(plan[1] - plan[0])
    return ((places >= plan[2]) & (places < plan[3])).astype(jnp.float32)


def coarse_tile(padded, own_panels, stiff_block, shift_first, shift_second):
    plan_first = window_plan(shift_first, own_panels.shape[2])
    plan_second = window_plan(shift_second, own_panels.shape[3])
    window = padded[:, :, plan_first[0] : plan_first[1], plan_second[0] : plan_second[1], :]
    keep_first = select_mask(plan_first)
    keep_second = select_mask(plan_second)
    masked = window * (keep_first[:, None, None] * keep_second[None, :, None])
    imaged = apply_stencil(
        masked, stiff_block[plan_first[4] : plan_first[5], plan_second[4] : plan_second[5], :]
    )
    panel_part = own_panels[:, :, plan_first[4] : plan_first[5], plan_second[4] : plan_second[5], :]
    return jnp.einsum("kabcd,labcd->kl", panel_part, imaged, precision=precise)


def jacobi(ext_residual, ext_stiff):
    inv_diag = damping / (26.0 + ext_stiff)
    correction = inv_diag * ext_residual
    for _ in range(SWEEPS - 1):
        widened = jnp.pad(correction, ((0, 0), (1, 1), (1, 1), (0, 0)))
        correction = correction + inv_diag * (ext_residual - apply_stencil(widened, ext_stiff))
    return correction


def inside_grid(cells_first, cells_second):
    keep = []
    for axis, length in (("gx", cells_first), ("gy", cells_second)):
        index, size = lax.axis_index(axis), lax.axis_size(axis)
        places = jnp.arange(length + 2)
        low = jnp.where(index == 0, 1, 0)
        high = jnp.where(index == size - 1, length, length + 1)
        keep.append(((places >= low) & (places <= high)).astype(jnp.float32))
    return keep[0][:, None, None] * keep[1][None, :, None]


def fold_axis(spread, dimension, length):
    interior = lax.slice_in_dim(spread, 2, 2 + length, axis=dimension)
    lower_part = lax.slice_in_dim(spread, 0, 1, axis=dimension)
    upper_part = lax.slice_in_dim(spread, length + 3, length + 4, axis=dimension)
    pads_low = [(0, 0)] * spread.ndim
    pads_high = [(0, 0)] * spread.ndim
    pads_low[dimension] = (0, length - 1)
    pads_high[dimension] = (length - 1, 0)
    return interior + jnp.pad(lower_part, pads_low) + jnp.pad(upper_part, pads_high)


def per_device_body(right_side, stiffness, panels):
    cells_first = stiffness.shape[0]
    cells_second = stiffness.shape[1]
    stiff_lifted = jnp.broadcast_to(stiffness[None, None], (1, 3) + stiffness.shape)
    padded, stiff_wide, right_wide = with_halo_stacked((panels, stiff_lifted, right_side[None]), 1)
    ext_stiff = stiff_wide[0, 0]
    ext_right = right_wide[0]
    own_wide = jnp.pad(panels, ((0, 0), (0, 0), (1, 1), (1, 1), (0, 0)))
    diag_tile = coarse_tile(own_wide, panels, stiffness, 0, 0)
    tile_list = [
        coarse_tile(padded, panels, stiffness, shift_first, shift_second)
        for shift_first, shift_second in neighbours
    ]
    weights = damping / jnp.diagonal(diag_tile)

    def precondition(current, ext_residual=None):
        restricted = jnp.einsum("kabcd,abcd->k", panels, current, precision=precise)
        first_guess = weights * restricted
        nearby = with_halo(first_guess[None, None], (("gx", 0), ("gy", 1)), 1)
        applied = jnp.dot(diag_tile, first_guess, precision=precise)
        for place, (shift_first, shift_second) in enumerate(neighbours):
            applied = applied + jnp.dot(
                tile_list[place], nearby[1 + shift_first, 1 + shift_second], precision=precise
            )
        coarse_vec = first_guess + weights * (restricted - applied)
        coarse_part = jnp.einsum("k,kabcd->abcd", coarse_vec, panels, precision=precise)
        if ext_residual is None:
            ext_residual = with_halo(current, (("gx", 1), ("gy", 2)), 1)
        correction = jacobi(ext_residual, ext_stiff)
        spread = with_halo(correction, (("gx", 1), ("gy", 2)), 1)
        folded = fold_axis(fold_axis(spread, 1, cells_first), 2, cells_second)
        return folded + coarse_part

    def operate(field):
        return apply_stencil(with_halo(field, (("gx", 1), ("gy", 2)), 1), stiffness)

    residual = right_side
    precond = precondition(residual, ext_right)
    ext_imaged = apply_stencil(with_halo(precond, (("gx", 1), ("gy", 2)), 2), ext_stiff)
    ext_imaged = ext_imaged * inside_grid(cells_first, cells_second)
    imaged = ext_imaged[:, 1:-1, 1:-1, :]
    smoothed = precondition(imaged, ext_imaged)
    twice = operate(smoothed)
    local_dots = jnp.stack(
        [
            jnp.sum(residual * precond),
            jnp.sum(precond * imaged),
            jnp.sum(residual * smoothed),
            jnp.sum(imaged * smoothed),
            jnp.sum(precond * twice),
            jnp.sum(smoothed * twice),
        ]
    )
    fit, curve, cross_r, cross_q, cross_z, curve_w = butterfly_sum(local_dots, ("gx", "gy"))
    step_first = fit / curve
    solution = step_first * precond
    residual = residual - step_first * imaged
    fit_next = fit - step_first * (curve + cross_r) + step_first * step_first * cross_q
    ratio = fit_next / fit
    grown = 1.0 + ratio
    curve_next = (
        grown * grown * curve
        - step_first * grown * (cross_z + cross_q)
        + step_first * step_first * curve_w
    )
    step_second = fit_next / curve_next
    precond_next = precond - step_first * smoothed
    direction = precond_next + ratio * precond
    imaged_next = (imaged - step_first * twice) + ratio * imaged
    solution = solution + step_second * direction
    residual = residual - step_second * imaged_next
    coupling = jnp.stack(tile_list).reshape(1, 1, 8, -1)
    return (solution, residual, coupling)


def solution(mesh):
    return jax.shard_map(
        per_device_body,
        mesh=mesh,
        in_specs=(P(None, "gx", "gy", None), P("gx", "gy", None), P(None, None, "gx", "gy", None)),
        out_specs=(P(None, "gx", "gy", None), P(None, "gx", "gy", None), P("gx", "gy", None, None)),
        check_vma=False,
    )
```

```python
import jax
import jax.numpy as jnp
from jax import lax
from jax.sharding import PartitionSpec as P

SWEEPS = 4


precise = lax.Precision.HIGHEST
mixing = 0.25
damping = 0.5
neighbours = ((-1, -1), (-1, 0), (-1, 1), (0, -1), (0, 1), (1, -1), (1, 0), (1, 1))


def with_halo(value, sides, width):
    for axis, dim in sides:
      size, length = (lax.axis_size(axis), value.shape[dim])
      up = [(i, (i + 1) % size) for i in range(size - 1)]
      down = [(j, i) for i, j in up]
      last = lax.slice_in_dim(value, length - width, length, axis=dim)
      initial = lax.slice_in_dim(value, 0, width, axis=dim)
      before = lax.ppermute(last, axis, up)
      after = lax.ppermute(initial, axis, down)
      value = jnp.concatenate([before, value, after], axis=dim)
    return value


def with_halo_stacked(arrays, width, dims, stack):
    arrays = list(arrays)
    for axis, dim in zip(("gx", "gy"), dims):
        size, length = lax.axis_size(axis), arrays[0].shape[dim]
        up = [(i, (i + 1) % size) for i in range(size - 1)]
        down = [(j, i) for i, j in up]
        lasts = [lax.slice_in_dim(a, length - width, length, axis=dim) for a in arrays]
        initials = [lax.slice_in_dim(a, 0, width, axis=dim) for a in arrays]
        before_all = lax.ppermute(jnp.concatenate(lasts, axis=stack), axis, up)
        after_all = lax.ppermute(jnp.concatenate(initials, axis=stack), axis, down)
        offset = 0
        for index, a in enumerate(arrays):
            count = a.shape[stack]
            before = lax.slice_in_dim(before_all, offset, offset + count, axis=stack)
            after = lax.slice_in_dim(after_all, offset, offset + count, axis=stack)
            offset += count
            arrays[index] = jnp.concatenate([before, a, after], axis=dim)
    return arrays


def butterfly_sum(value, axes):
    for axis in axes:
        size = lax.axis_size(axis)
        stride = 1
        while stride < size:
            partners = [(i, i ^ stride) for i in range(size)]
            value = value + lax.ppermute(value, axis, partners)
            stride *= 2
    return value


def apply_stencil(window, stiff_block):
    paddings = [(0, 0)] * (window.ndim - 1) + [(1, 1)]
    widened = jnp.pad(window, paddings)
    along_first = widened[..., :-2, :, :] + widened[..., 1:-1, :, :] + widened[..., 2:, :, :]
    along_second = (
        along_first[..., :, :-2, :] + along_first[..., :, 1:-1, :] + along_first[..., :, 2:, :]
    )
    box_sum = along_second[..., :-2] + along_second[..., 1:-1] + along_second[..., 2:]
    centre = window[..., 1:-1, 1:-1, :]
    slope_first = widened[..., 2:, :, :] - widened[..., :-2, :, :]
    slope_second = widened[..., 1:-1, 2:, :] - widened[..., 1:-1, :-2, :]
    mixed_ab = slope_first[..., :, 2:, 1:-1] - slope_first[..., :, :-2, 1:-1]
    mixed_ac = slope_first[..., :, 1:-1, 2:] - slope_first[..., :, 1:-1, :-2]
    mixed_bc = slope_second[..., 2:] - slope_second[..., :-2]
    cross_terms = jnp.stack(
        [
            mixed_ab[..., 1, :, :, :] + mixed_ac[..., 2, :, :, :],
            mixed_ab[..., 0, :, :, :] + mixed_bc[..., 2, :, :, :],
            mixed_ac[..., 0, :, :, :] + mixed_bc[..., 1, :, :, :],
        ],
        axis=-4,
    )
    return (27.0 + stiff_block) * centre - box_sum + mixing * cross_terms


def apply_stencil_minor(window, stiff_block):
    widened = jnp.pad(window, ((0, 0), (0, 0), (0, 0), (0, 0), (1, 1)))
    along_first = widened[:, :-2] + widened[:, 1:-1] + widened[:, 2:]
    along_second = along_first[:, :, :-2] + along_first[:, :, 1:-1] + along_first[:, :, 2:]
    box_sum = along_second[..., :-2] + along_second[..., 1:-1] + along_second[..., 2:]
    centre = window[:, 1:-1, 1:-1]
    slope_first = widened[:, 2:] - widened[:, :-2]
    slope_second = widened[:, 1:-1, 2:] - widened[:, 1:-1, :-2]
    mixed_ab = slope_first[:, :, 2:, :, 1:-1] - slope_first[:, :, :-2, :, 1:-1]
    mixed_ac = slope_first[:, :, 1:-1, :, 2:] - slope_first[:, :, 1:-1, :, :-2]
    mixed_bc = slope_second[..., 2:] - slope_second[..., :-2]
    cross_terms = jnp.stack(
        [
            mixed_ab[1] + mixed_ac[2],
            mixed_ab[0] + mixed_bc[2],
            mixed_ac[0] + mixed_bc[1],
        ],
        axis=0,
    )
    return (27.0 + stiff_block[:, :, None, :]) * centre - box_sum + mixing * cross_terms


def coarse_tile_minor(padded, own_panels, stiff_block, shift_first, shift_second):
    plan_first = window_plan(shift_first, own_panels.shape[1])
    plan_second = window_plan(shift_second, own_panels.shape[2])
    window = padded[:, plan_first[0] : plan_first[1], plan_second[0] : plan_second[1]]
    keep_first = select_mask(plan_first)
    keep_second = select_mask(plan_second)
    masked = window * (keep_first[:, None, None, None] * keep_second[None, :, None, None])
    imaged = apply_stencil_minor(
        masked, stiff_block[plan_first[4] : plan_first[5], plan_second[4] : plan_second[5], :]
    )
    panel_part = own_panels[:, plan_first[4] : plan_first[5], plan_second[4] : plan_second[5]]
    return jnp.einsum("abckd,abcld->kl", panel_part, imaged, precision=precise)


def window_plan(offset, length):
    if offset == 0:
        return (0, length + 2, 1, length + 1, 0, length)
    if offset == 1:
        return (length - 1, length + 2, 2, 3, length - 1, length)
    return (0, 3, 0, 1, 0, 1)


def select_mask(plan):
    places = jnp.arange(plan[1] - plan[0])
    return ((places >= plan[2]) & (places < plan[3])).astype(jnp.float32)


def jacobi(ext_residual, ext_stiff):
    inv_diag = damping / (26.0 + ext_stiff)
    correction = inv_diag * ext_residual
    for _ in range(SWEEPS - 1):
        widened = jnp.pad(correction, ((0, 0), (1, 1), (1, 1), (0, 0)))
        correction = correction + inv_diag * (ext_residual - apply_stencil(widened, ext_stiff))
    return correction


def inside_grid(cells_first, cells_second):
    keep = []
    for axis, length in (("gx", cells_first), ("gy", cells_second)):
        index, size = lax.axis_index(axis), lax.axis_size(axis)
        places = jnp.arange(length + 2)
        low = jnp.where(index == 0, 1, 0)
        high = jnp.where(index == size - 1, length, length + 1)
        keep.append(((places >= low) & (places <= high)).astype(jnp.float32))
    return keep[0][:, None, None] * keep[1][None, :, None]


def fold_axis(spread, dimension, length):
    interior = lax.slice_in_dim(spread, 2, 2 + length, axis=dimension)
    lower_part = lax.slice_in_dim(spread, 0, 1, axis=dimension)
    upper_part = lax.slice_in_dim(spread, length + 3, length + 4, axis=dimension)
    pads_low = [(0, 0)] * spread.ndim
    pads_high = [(0, 0)] * spread.ndim
    pads_low[dimension] = (0, length - 1)
    pads_high[dimension] = (length - 1, 0)
    return interior + jnp.pad(lower_part, pads_low) + jnp.pad(upper_part, pads_high)


def per_device_body(right_side, stiffness, panels):
    cells_first = stiffness.shape[0]
    cells_second = stiffness.shape[1]
    panels_minor = jnp.transpose(panels, (1, 2, 3, 0, 4))
    stiff_lifted = jnp.broadcast_to(
        stiffness[None, :, :, None, :], (3, cells_first, cells_second, 1, stiffness.shape[2])
    )
    padded, stiff_wide, right_wide = with_halo_stacked(
        (panels_minor, stiff_lifted, right_side[:, :, :, None, :]), 1, (1, 2), 3
    )
    ext_stiff = stiff_wide[0, :, :, 0, :]
    ext_right = right_wide[:, :, :, 0, :]
    own_wide = jnp.pad(panels_minor, ((0, 0), (1, 1), (1, 1), (0, 0), (0, 0)))
    diag_tile = coarse_tile_minor(own_wide, panels_minor, stiffness, 0, 0)
    tile_list = [
        coarse_tile_minor(padded, panels_minor, stiffness, shift_first, shift_second)
        for shift_first, shift_second in neighbours
    ]
    weights = damping / jnp.diagonal(diag_tile)

    def precondition(current, ext_residual=None):
        restricted = jnp.einsum("kabcd,abcd->k", panels, current, precision=precise)
        first_guess = weights * restricted
        nearby = with_halo(first_guess[None, None], (("gx", 0), ("gy", 1)), 1)
        applied = jnp.dot(diag_tile, first_guess, precision=precise)
        for place, (shift_first, shift_second) in enumerate(neighbours):
            applied = applied + jnp.dot(
                tile_list[place], nearby[1 + shift_first, 1 + shift_second], precision=precise
            )
        coarse_vec = first_guess + weights * (restricted - applied)
        coarse_part = jnp.einsum("k,kabcd->abcd", coarse_vec, panels, precision=precise)
        if ext_residual is None:
            ext_residual = with_halo(current, (("gx", 1), ("gy", 2)), 1)
        correction = jacobi(ext_residual, ext_stiff)
        spread = with_halo(correction, (("gx", 1), ("gy", 2)), 1)
        folded = fold_axis(fold_axis(spread, 1, cells_first), 2, cells_second)
        return folded + coarse_part

    def operate(field):
        return apply_stencil(with_halo(field, (("gx", 1), ("gy", 2)), 1), stiffness)

    residual = right_side
    precond = precondition(residual, ext_right)
    ext_imaged = apply_stencil(with_halo(precond, (("gx", 1), ("gy", 2)), 2), ext_stiff)
    ext_imaged = ext_imaged * inside_grid(cells_first, cells_second)
    imaged = ext_imaged[:, 1:-1, 1:-1, :]
    smoothed = precondition(imaged, ext_imaged)
    twice = operate(smoothed)
    local_dots = jnp.stack(
        [
            jnp.sum(residual * precond),
            jnp.sum(precond * imaged),
            jnp.sum(residual * smoothed),
            jnp.sum(imaged * smoothed),
            jnp.sum(precond * twice),
            jnp.sum(smoothed * twice),
        ]
    )
    fit, curve, cross_r, cross_q, cross_z, curve_w = butterfly_sum(local_dots, ("gx", "gy"))
    step_first = fit / curve
    solution = step_first * precond
    residual = residual - step_first * imaged
    fit_next = fit - step_first * (curve + cross_r) + step_first * step_first * cross_q
    ratio = fit_next / fit
    grown = 1.0 + ratio
    curve_next = (
        grown * grown * curve
        - step_first * grown * (cross_z + cross_q)
        + step_first * step_first * curve_w
    )
    step_second = fit_next / curve_next
    precond_next = precond - step_first * smoothed
    direction = precond_next + ratio * precond
    imaged_next = (imaged - step_first * twice) + ratio * imaged
    solution = solution + step_second * direction
    residual = residual - step_second * imaged_next
    coupling = jnp.stack(tile_list).reshape(1, 1, 8, -1)
    return (solution, residual, coupling)


def solution(mesh):
    return jax.shard_map(
        per_device_body,
        mesh=mesh,
        in_specs=(P(None, "gx", "gy", None), P("gx", "gy", None), P(None, None, "gx", "gy", None)),
        out_specs=(P(None, "gx", "gy", None), P(None, "gx", "gy", None), P("gx", "gy", None, None)),
        check_vma=False,
    )
```

```python
import jax
import jax.numpy as jnp
from jax import lax
from jax.sharding import PartitionSpec as P

SWEEPS = 4


precise = lax.Precision.HIGHEST
mixing = 0.25
damping = 0.5
neighbours = ((-1, -1), (-1, 0), (-1, 1), (0, -1), (0, 1), (1, -1), (1, 0), (1, 1))


def with_halo(value, sides, width):
    for axis, dim in sides:
      size, length = (lax.axis_size(axis), value.shape[dim])
      up = [(i, (i + 1) % size) for i in range(size - 1)]
      down = [(j, i) for i, j in up]
      last = lax.slice_in_dim(value, length - width, length, axis=dim)
      initial = lax.slice_in_dim(value, 0, width, axis=dim)
      before = lax.ppermute(last, axis, up)
      after = lax.ppermute(initial, axis, down)
      value = jnp.concatenate([before, value, after], axis=dim)
    return value


def with_halo_stacked(arrays, width):
    arrays = list(arrays)
    for axis, dim in (("gx", 2), ("gy", 3)):
        size, length = lax.axis_size(axis), arrays[0].shape[dim]
        up = [(i, (i + 1) % size) for i in range(size - 1)]
        down = [(j, i) for i, j in up]
        lasts = [lax.slice_in_dim(a, length - width, length, axis=dim) for a in arrays]
        initials = [lax.slice_in_dim(a, 0, width, axis=dim) for a in arrays]
        before_all = lax.ppermute(jnp.concatenate(lasts, axis=0), axis, up)
        after_all = lax.ppermute(jnp.concatenate(initials, axis=0), axis, down)
        offset = 0
        for index, a in enumerate(arrays):
            count = a.shape[0]
            before = before_all[offset : offset + count]
            after = after_all[offset : offset + count]
            offset += count
            arrays[index] = jnp.concatenate([before, a, after], axis=dim)
    return arrays


def butterfly_sum(value, axes):
    for axis in axes:
        size = lax.axis_size(axis)
        stride = 1
        while stride < size:
            partners = [(i, i ^ stride) for i in range(size)]
            value = value + lax.ppermute(value, axis, partners)
            stride *= 2
    return value


def apply_stencil(window, stiff_block):
    paddings = [(0, 0)] * (window.ndim - 1) + [(1, 1)]
    widened = jnp.pad(window, paddings)
    along_first = widened[..., :-2, :, :] + widened[..., 1:-1, :, :] + widened[..., 2:, :, :]
    along_second = (
        along_first[..., :, :-2, :] + along_first[..., :, 1:-1, :] + along_first[..., :, 2:, :]
    )
    box_sum = along_second[..., :-2] + along_second[..., 1:-1] + along_second[..., 2:]
    centre = window[..., 1:-1, 1:-1, :]
    slope_first = widened[..., 2:, :, :] - widened[..., :-2, :, :]
    slope_second = widened[..., 1:-1, 2:, :] - widened[..., 1:-1, :-2, :]
    mixed_ab = slope_first[..., :, 2:, 1:-1] - slope_first[..., :, :-2, 1:-1]
    mixed_ac = slope_first[..., :, 1:-1, 2:] - slope_first[..., :, 1:-1, :-2]
    mixed_bc = slope_second[..., 2:] - slope_second[..., :-2]
    cross_terms = jnp.stack(
        [
            mixed_ab[..., 1, :, :, :] + mixed_ac[..., 2, :, :, :],
            mixed_ab[..., 0, :, :, :] + mixed_bc[..., 2, :, :, :],
            mixed_ac[..., 0, :, :, :] + mixed_bc[..., 1, :, :, :],
        ],
        axis=-4,
    )
    return (27.0 + stiff_block) * centre - box_sum + mixing * cross_terms


def window_plan(offset, length):
    if offset == 0:
        return (0, length + 2, 1, length + 1, 0, length)
    if offset == 1:
        return (length - 1, length + 2, 2, 3, length - 1, length)
    return (0, 3, 0, 1, 0, 1)


def select_mask(plan):
    places = jnp.arange(plan[1] - plan[0])
    return ((places >= plan[2]) & (places < plan[3])).astype(jnp.float32)


def coarse_tile(padded, own_panels, stiff_block, shift_first, shift_second):
    plan_first = window_plan(shift_first, own_panels.shape[2])
    plan_second = window_plan(shift_second, own_panels.shape[3])
    window = padded[:, :, plan_first[0] : plan_first[1], plan_second[0] : plan_second[1], :]
    keep_first = select_mask(plan_first)
    keep_second = select_mask(plan_second)
    masked = window * (keep_first[:, None, None] * keep_second[None, :, None])
    imaged = apply_stencil(
        masked, stiff_block[plan_first[4] : plan_first[5], plan_second[4] : plan_second[5], :]
    )
    panel_part = own_panels[:, :, plan_first[4] : plan_first[5], plan_second[4] : plan_second[5], :]
    return jnp.einsum("kabcd,labcd->kl", panel_part, imaged, precision=precise)


def jacobi(ext_residual, ext_stiff):
    inv_diag = damping / (26.0 + ext_stiff)
    correction = inv_diag * ext_residual
    for _ in range(SWEEPS - 1):
        widened = jnp.pad(correction, ((0, 0), (1, 1), (1, 1), (0, 0)))
        correction = correction + inv_diag * (ext_residual - apply_stencil(widened, ext_stiff))
    return correction


def inside_grid(cells_first, cells_second):
    keep = []
    for axis, length in (("gx", cells_first), ("gy", cells_second)):
        index, size = lax.axis_index(axis), lax.axis_size(axis)
        places = jnp.arange(length + 2)
        low = jnp.where(index == 0, 1, 0)
        high = jnp.where(index == size - 1, length, length + 1)
        keep.append(((places >= low) & (places <= high)).astype(jnp.float32))
    return keep[0][:, None, None] * keep[1][None, :, None]


def fold_axis(spread, dimension, length):
    interior = lax.slice_in_dim(spread, 2, 2 + length, axis=dimension)
    lower_part = lax.slice_in_dim(spread, 0, 1, axis=dimension)
    upper_part = lax.slice_in_dim(spread, length + 3, length + 4, axis=dimension)
    pads_low = [(0, 0)] * spread.ndim
    pads_high = [(0, 0)] * spread.ndim
    pads_low[dimension] = (0, length - 1)
    pads_high[dimension] = (length - 1, 0)
    return interior + jnp.pad(lower_part, pads_low) + jnp.pad(upper_part, pads_high)


def per_device_body(right_side, stiffness, panels):
    cells_first = stiffness.shape[0]
    cells_second = stiffness.shape[1]
    stiff_lifted = jnp.broadcast_to(stiffness[None, None], (1, 3) + stiffness.shape)
    padded, stiff_wide, right_wide = with_halo_stacked((panels, stiff_lifted, right_side[None]), 1)
    ext_stiff = stiff_wide[0, 0]
    ext_right = right_wide[0]
    own_wide = jnp.pad(panels, ((0, 0), (0, 0), (1, 1), (1, 1), (0, 0)))
    diag_tile = coarse_tile(own_wide, panels, stiffness, 0, 0)
    tile_list = []
    for shift_first, shift_second in neighbours:
        tile_list.append(coarse_tile(padded, panels, stiffness, shift_first, shift_second))
    weights = damping / jnp.diagonal(diag_tile)

    def precondition(current, ext_residual=None):
        restricted = jnp.einsum("kabcd,abcd->k", panels, current, precision=precise)
        first_guess = weights * restricted
        nearby = with_halo(first_guess[None, None], (("gx", 0), ("gy", 1)), 1)
        applied = jnp.dot(diag_tile, first_guess, precision=precise)
        for place, (shift_first, shift_second) in enumerate(neighbours):
            applied = applied + jnp.dot(
                tile_list[place], nearby[1 + shift_first, 1 + shift_second], precision=precise
            )
        coarse_vec = first_guess + weights * (restricted - applied)
        coarse_part = jnp.einsum("k,kabcd->abcd", coarse_vec, panels, precision=precise)
        if ext_residual is None:
            ext_residual = with_halo(current, (("gx", 1), ("gy", 2)), 1)
        correction = jacobi(ext_residual, ext_stiff)
        spread = with_halo(correction, (("gx", 1), ("gy", 2)), 1)
        folded = fold_axis(fold_axis(spread, 1, cells_first), 2, cells_second)
        return folded + coarse_part

    def operate(field):
        return apply_stencil(with_halo(field, (("gx", 1), ("gy", 2)), 1), stiffness)

    residual = right_side
    precond = precondition(residual, ext_right)
    ext_imaged = apply_stencil(with_halo(precond, (("gx", 1), ("gy", 2)), 2), ext_stiff)
    ext_imaged = ext_imaged * inside_grid(cells_first, cells_second)
    imaged = ext_imaged[:, 1:-1, 1:-1, :]
    smoothed = precondition(imaged, ext_imaged)
    twice = operate(smoothed)
    local_dots = jnp.stack(
        [
            jnp.sum(residual * precond),
            jnp.sum(precond * imaged),
            jnp.sum(residual * smoothed),
            jnp.sum(imaged * smoothed),
            jnp.sum(precond * twice),
            jnp.sum(smoothed * twice),
        ]
    )
    fit, curve, cross_r, cross_q, cross_z, curve_w = butterfly_sum(local_dots, ("gx", "gy"))
    step_first = fit / curve
    solution = step_first * precond
    residual = residual - step_first * imaged
    fit_next = fit - step_first * (curve + cross_r) + step_first * step_first * cross_q
    ratio = fit_next / fit
    grown = 1.0 + ratio
    curve_next = (
        grown * grown * curve
        - step_first * grown * (cross_z + cross_q)
        + step_first * step_first * curve_w
    )
    step_second = fit_next / curve_next
    precond_next = precond - step_first * smoothed
    direction = precond_next + ratio * precond
    imaged_next = (imaged - step_first * twice) + ratio * imaged
    solution = solution + step_second * direction
    residual = residual - step_second * imaged_next
    coupling = jnp.stack(tile_list).reshape(1, 1, 8, -1)
    return (solution, residual, coupling)


def solution(mesh):
    return jax.shard_map(
        per_device_body,
        mesh=mesh,
        in_specs=(P(None, "gx", "gy", None), P("gx", "gy", None), P(None, None, "gx", "gy", None)),
        out_specs=(P(None, "gx", "gy", None), P(None, "gx", "gy", None), P("gx", "gy", None, None)),
        check_vma=False,
    )
```

```python
import jax
import jax.numpy as jnp
from jax import lax
from jax.sharding import PartitionSpec as P

SWEEPS = 4


precise = lax.Precision.HIGHEST
mixing = 0.25
damping = 0.5
neighbours = ((-1, -1), (-1, 0), (-1, 1), (0, -1), (0, 1), (1, -1), (1, 0), (1, 1))


def with_halo(value, sides, width):
    for axis, dim in sides:
      size, length = (lax.axis_size(axis), value.shape[dim])
      up = [(i, (i + 1) % size) for i in range(size - 1)]
      down = [(j, i) for i, j in up]
      last = lax.slice_in_dim(value, length - width, length, axis=dim)
      initial = lax.slice_in_dim(value, 0, width, axis=dim)
      before = lax.ppermute(last, axis, up)
      after = lax.ppermute(initial, axis, down)
      value = jnp.concatenate([before, value, after], axis=dim)
    return value


def with_halo_stacked(arrays, width):
    arrays = list(arrays)
    for axis, dim in (("gx", 2), ("gy", 3)):
        size, length = lax.axis_size(axis), arrays[0].shape[dim]
        up = [(i, (i + 1) % size) for i in range(size - 1)]
        down = [(j, i) for i, j in up]
        lasts = [lax.slice_in_dim(a, length - width, length, axis=dim) for a in arrays]
        initials = [lax.slice_in_dim(a, 0, width, axis=dim) for a in arrays]
        before_all = lax.ppermute(jnp.concatenate(lasts, axis=0), axis, up)
        after_all = lax.ppermute(jnp.concatenate(initials, axis=0), axis, down)
        offset = 0
        for index, a in enumerate(arrays):
            count = a.shape[0]
            before = before_all[offset : offset + count]
            after = after_all[offset : offset + count]
            offset += count
            arrays[index] = jnp.concatenate([before, a, after], axis=dim)
    return arrays


def mirror_sum(value):
    size_first, size_second = lax.axis_size("gx"), lax.axis_size("gy")
    steps = ((0, 1), (1, 0), (2, 0), (6, 0), (0, 2), (0, 6), (1, 8))
    for flip_first, flip_second in steps:
        partners = [
            (a * size_second + b, (a ^ flip_first) * size_second + (b ^ flip_second))
            for a in range(size_first)
            for b in range(size_second)
        ]
        value = value + lax.ppermute(value, ("gx", "gy"), partners)
    return value


def apply_stencil(window, stiff_block):
    paddings = [(0, 0)] * (window.ndim - 1) + [(1, 1)]
    widened = jnp.pad(window, paddings)
    along_first = widened[..., :-2, :, :] + widened[..., 1:-1, :, :] + widened[..., 2:, :, :]
    along_second = (
        along_first[..., :, :-2, :] + along_first[..., :, 1:-1, :] + along_first[..., :, 2:, :]
    )
    box_sum = along_second[..., :-2] + along_second[..., 1:-1] + along_second[..., 2:]
    centre = window[..., 1:-1, 1:-1, :]
    slope_first = widened[..., 2:, :, :] - widened[..., :-2, :, :]
    slope_second = widened[..., 1:-1, 2:, :] - widened[..., 1:-1, :-2, :]
    mixed_ab = slope_first[..., :, 2:, 1:-1] - slope_first[..., :, :-2, 1:-1]
    mixed_ac = slope_first[..., :, 1:-1, 2:] - slope_first[..., :, 1:-1, :-2]
    mixed_bc = slope_second[..., 2:] - slope_second[..., :-2]
    cross_terms = jnp.stack(
        [
            mixed_ab[..., 1, :, :, :] + mixed_ac[..., 2, :, :, :],
            mixed_ab[..., 0, :, :, :] + mixed_bc[..., 2, :, :, :],
            mixed_ac[..., 0, :, :, :] + mixed_bc[..., 1, :, :, :],
        ],
        axis=-4,
    )
    return (27.0 + stiff_block) * centre - box_sum + mixing * cross_terms


def window_plan(offset, length):
    if offset == 0:
        return (0, length + 2, 1, length + 1, 0, length)
    if offset == 1:
        return (length - 1, length + 2, 2, 3, length - 1, length)
    return (0, 3, 0, 1, 0, 1)


def select_mask(plan):
    places = jnp.arange(plan[1] - plan[0])
    return ((places >= plan[2]) & (places < plan[3])).astype(jnp.float32)


def coarse_tile(padded, own_panels, stiff_block, shift_first, shift_second):
    plan_first = window_plan(shift_first, own_panels.shape[2])
    plan_second = window_plan(shift_second, own_panels.shape[3])
    window = padded[:, :, plan_first[0] : plan_first[1], plan_second[0] : plan_second[1], :]
    keep_first = select_mask(plan_first)
    keep_second = select_mask(plan_second)
    masked = window * (keep_first[:, None, None] * keep_second[None, :, None])
    imaged = apply_stencil(
        masked, stiff_block[plan_first[4] : plan_first[5], plan_second[4] : plan_second[5], :]
    )
    panel_part = own_panels[:, :, plan_first[4] : plan_first[5], plan_second[4] : plan_second[5], :]
    return jnp.einsum("kabcd,labcd->kl", panel_part, imaged, precision=precise)


def jacobi(ext_residual, ext_stiff):
    inv_diag = damping / (26.0 + ext_stiff)
    correction = inv_diag * ext_residual
    for _ in range(SWEEPS - 1):
        widened = jnp.pad(correction, ((0, 0), (1, 1), (1, 1), (0, 0)))
        correction = correction + inv_diag * (ext_residual - apply_stencil(widened, ext_stiff))
    return correction


def inside_grid(cells_first, cells_second):
    keep = []
    for axis, length in (("gx", cells_first), ("gy", cells_second)):
        index, size = lax.axis_index(axis), lax.axis_size(axis)
        places = jnp.arange(length + 2)
        low = jnp.where(index == 0, 1, 0)
        high = jnp.where(index == size - 1, length, length + 1)
        keep.append(((places >= low) & (places <= high)).astype(jnp.float32))
    return keep[0][:, None, None] * keep[1][None, :, None]


def fold_axis(spread, dimension, length):
    interior = lax.slice_in_dim(spread, 2, 2 + length, axis=dimension)
    lower_part = lax.slice_in_dim(spread, 0, 1, axis=dimension)
    upper_part = lax.slice_in_dim(spread, length + 3, length + 4, axis=dimension)
    pads_low = [(0, 0)] * spread.ndim
    pads_high = [(0, 0)] * spread.ndim
    pads_low[dimension] = (0, length - 1)
    pads_high[dimension] = (length - 1, 0)
    return interior + jnp.pad(lower_part, pads_low) + jnp.pad(upper_part, pads_high)


def per_device_body(right_side, stiffness, panels):
    cells_first = stiffness.shape[0]
    cells_second = stiffness.shape[1]
    stiff_lifted = jnp.broadcast_to(stiffness[None, None], (1, 3) + stiffness.shape)
    padded, stiff_wide, right_wide = with_halo_stacked((panels, stiff_lifted, right_side[None]), 1)
    ext_stiff = stiff_wide[0, 0]
    ext_right = right_wide[0]
    own_wide = jnp.pad(panels, ((0, 0), (0, 0), (1, 1), (1, 1), (0, 0)))
    diag_tile = coarse_tile(own_wide, panels, stiffness, 0, 0)
    tile_list = [
        coarse_tile(padded, panels, stiffness, shift_first, shift_second)
        for shift_first, shift_second in neighbours
    ]
    weights = damping / jnp.diagonal(diag_tile)

    def precondition(current, ext_residual=None):
        restricted = jnp.einsum("kabcd,abcd->k", panels, current, precision=precise)
        first_guess = weights * restricted
        if ext_residual is None:
            ext_residual = with_halo(current, (("gx", 1), ("gy", 2)), 1)
        correction = jacobi(ext_residual, ext_stiff)
        rows, cols = correction.shape[1], correction.shape[2]
        carrier = jnp.zeros((1,) + correction.shape[1:], correction.dtype)
        for row in (0, rows - 1):
            for col in (0, cols - 1):
                carrier = carrier.at[0, row, col, : first_guess.shape[0]].set(first_guess)
        spread_all = with_halo(
            jnp.concatenate([correction, carrier], axis=0), (("gx", 1), ("gy", 2)), 1
        )
        spread, carried = spread_all[:3], spread_all[3]
        place_row = {-1: 0, 0: 1, 1: rows + 1}
        place_col = {-1: 0, 0: 1, 1: cols + 1}
        applied = jnp.dot(diag_tile, first_guess, precision=precise)
        for place, (shift_first, shift_second) in enumerate(neighbours):
            guess = carried[place_row[shift_first], place_col[shift_second], : first_guess.shape[0]]
            applied = applied + jnp.dot(tile_list[place], guess, precision=precise)
        coarse_vec = first_guess + weights * (restricted - applied)
        coarse_part = jnp.einsum("k,kabcd->abcd", coarse_vec, panels, precision=precise)
        folded = fold_axis(fold_axis(spread, 1, cells_first), 2, cells_second)
        return folded + coarse_part

    def operate(field):
        return apply_stencil(with_halo(field, (("gx", 1), ("gy", 2)), 1), stiffness)

    residual = right_side
    precond = precondition(residual, ext_right)
    ext_imaged = apply_stencil(with_halo(precond, (("gx", 1), ("gy", 2)), 2), ext_stiff)
    ext_imaged = ext_imaged * inside_grid(cells_first, cells_second)
    imaged = ext_imaged[:, 1:-1, 1:-1, :]
    smoothed = precondition(imaged, ext_imaged)
    twice = operate(smoothed)
    local_dots = jnp.stack(
        [
            jnp.sum(residual * precond),
            jnp.sum(precond * imaged),
            jnp.sum(residual * smoothed),
            jnp.sum(imaged * smoothed),
            jnp.sum(precond * twice),
            jnp.sum(smoothed * twice),
        ]
    )
    fit, curve, cross_r, cross_q, cross_z, curve_w = mirror_sum(local_dots)
    step_first = fit / curve
    solution = step_first * precond
    residual = residual - step_first * imaged
    fit_next = fit - step_first * (curve + cross_r) + step_first * step_first * cross_q
    ratio = fit_next / fit
    grown = 1.0 + ratio
    curve_next = (
        grown * grown * curve
        - step_first * grown * (cross_z + cross_q)
        + step_first * step_first * curve_w
    )
    step_second = fit_next / curve_next
    precond_next = precond - step_first * smoothed
    direction = precond_next + ratio * precond
    imaged_next = (imaged - step_first * twice) + ratio * imaged
    solution = solution + step_second * direction
    residual = residual - step_second * imaged_next
    coupling = jnp.stack(tile_list).reshape(1, 1, 8, -1)
    return (solution, residual, coupling)


def solution(mesh):
    return jax.shard_map(
        per_device_body,
        mesh=mesh,
        in_specs=(P(None, "gx", "gy", None), P("gx", "gy", None), P(None, None, "gx", "gy", None)),
        out_specs=(P(None, "gx", "gy", None), P(None, "gx", "gy", None), P("gx", "gy", None, None)),
        check_vma=False,
    )
```

```python
import jax
import jax.numpy as jnp
from jax import lax
from jax.sharding import PartitionSpec as P

SWEEPS = 4


precise = lax.Precision.HIGHEST
mixing = 0.25
damping = 0.5
neighbours = ((-1, -1), (-1, 0), (-1, 1), (0, -1), (0, 1), (1, -1), (1, 0), (1, 1))


def with_halo(value, sides, width):
    for axis, dim in sides:
      size, length = (lax.axis_size(axis), value.shape[dim])
      up = [(i, (i + 1) % size) for i in range(size - 1)]
      down = [(j, i) for i, j in up]
      last = lax.slice_in_dim(value, length - width, length, axis=dim)
      initial = lax.slice_in_dim(value, 0, width, axis=dim)
      before = lax.ppermute(last, axis, up)
      after = lax.ppermute(initial, axis, down)
      value = jnp.concatenate([before, value, after], axis=dim)
    return value


def with_halo_stacked(arrays, width):
    arrays = list(arrays)
    for axis, dim in (("gx", 2), ("gy", 3)):
        size, length = lax.axis_size(axis), arrays[0].shape[dim]
        up = [(i, (i + 1) % size) for i in range(size - 1)]
        down = [(j, i) for i, j in up]
        lasts = [lax.slice_in_dim(a, length - width, length, axis=dim) for a in arrays]
        initials = [lax.slice_in_dim(a, 0, width, axis=dim) for a in arrays]
        before_all = lax.ppermute(jnp.concatenate(lasts, axis=0), axis, up)
        after_all = lax.ppermute(jnp.concatenate(initials, axis=0), axis, down)
        offset = 0
        for index, a in enumerate(arrays):
            count = a.shape[0]
            before = before_all[offset : offset + count]
            after = after_all[offset : offset + count]
            offset += count
            arrays[index] = jnp.concatenate([before, a, after], axis=dim)
    return arrays


def butterfly_sum(value, axes):
    for axis in axes:
        size = lax.axis_size(axis)
        stride = 1
        while stride < size:
            partners = [(i, i ^ stride) for i in range(size)]
            value = value + lax.ppermute(value, axis, partners)
            stride *= 2
    return value


def apply_stencil(window, stiff_block):
    paddings = [(0, 0)] * (window.ndim - 1) + [(1, 1)]
    widened = jnp.pad(window, paddings)
    along_first = widened[..., :-2, :, :] + widened[..., 1:-1, :, :] + widened[..., 2:, :, :]
    along_second = (
        along_first[..., :, :-2, :] + along_first[..., :, 1:-1, :] + along_first[..., :, 2:, :]
    )
    box_sum = along_second[..., :-2] + along_second[..., 1:-1] + along_second[..., 2:]
    centre = window[..., 1:-1, 1:-1, :]
    slope_first = widened[..., 2:, :, :] - widened[..., :-2, :, :]
    slope_second = widened[..., 1:-1, 2:, :] - widened[..., 1:-1, :-2, :]
    mixed_ab = slope_first[..., :, 2:, 1:-1] - slope_first[..., :, :-2, 1:-1]
    mixed_ac = slope_first[..., :, 1:-1, 2:] - slope_first[..., :, 1:-1, :-2]
    mixed_bc = slope_second[..., 2:] - slope_second[..., :-2]
    cross_terms = jnp.stack(
        [
            mixed_ab[..., 1, :, :, :] + mixed_ac[..., 2, :, :, :],
            mixed_ab[..., 0, :, :, :] + mixed_bc[..., 2, :, :, :],
            mixed_ac[..., 0, :, :, :] + mixed_bc[..., 1, :, :, :],
        ],
        axis=-4,
    )
    return (27.0 + stiff_block) * centre - box_sum + mixing * cross_terms


def window_plan(offset, length):
    if offset == 0:
        return (0, length + 2, 1, length + 1, 0, length)
    if offset == 1:
        return (length - 1, length + 2, 2, 3, length - 1, length)
    return (0, 3, 0, 1, 0, 1)


def select_mask(plan):
    places = jnp.arange(plan[1] - plan[0])
    return ((places >= plan[2]) & (places < plan[3])).astype(jnp.float32)


def coarse_tile(padded, own_panels, stiff_block, shift_first, shift_second):
    plan_first = window_plan(shift_first, own_panels.shape[2])
    plan_second = window_plan(shift_second, own_panels.shape[3])
    window = padded[:, :, plan_first[0] : plan_first[1], plan_second[0] : plan_second[1], :]
    keep_first = select_mask(plan_first)
    keep_second = select_mask(plan_second)
    masked = window * (keep_first[:, None, None] * keep_second[None, :, None])
    imaged = apply_stencil(
        masked, stiff_block[plan_first[4] : plan_first[5], plan_second[4] : plan_second[5], :]
    )
    panel_part = own_panels[:, :, plan_first[4] : plan_first[5], plan_second[4] : plan_second[5], :]
    return jnp.einsum("kabcd,labcd->kl", panel_part, imaged, precision=precise)


def jacobi(ext_residual, ext_stiff):
    inv_diag = damping / (26.0 + ext_stiff)
    correction = inv_diag * ext_residual
    for _ in range(SWEEPS - 1):
        widened = jnp.pad(correction, ((0, 0), (1, 1), (1, 1), (0, 0)))
        correction = correction + inv_diag * (ext_residual - apply_stencil(widened, ext_stiff))
    return correction


def inside_grid(cells_first, cells_second):
    keep = []
    for axis, length in (("gx", cells_first), ("gy", cells_second)):
        index, size = lax.axis_index(axis), lax.axis_size(axis)
        places = jnp.arange(length + 2)
        low = jnp.where(index == 0, 1, 0)
        high = jnp.where(index == size - 1, length, length + 1)
        keep.append(((places >= low) & (places <= high)).astype(jnp.float32))
    return keep[0][:, None, None] * keep[1][None, :, None]


def fold_axis(spread, dimension, length):
    interior = lax.slice_in_dim(spread, 2, 2 + length, axis=dimension)
    lower_part = lax.slice_in_dim(spread, 0, 1, axis=dimension)
    upper_part = lax.slice_in_dim(spread, length + 3, length + 4, axis=dimension)
    pads_low = [(0, 0)] * spread.ndim
    pads_high = [(0, 0)] * spread.ndim
    pads_low[dimension] = (0, length - 1)
    pads_high[dimension] = (length - 1, 0)
    return interior + jnp.pad(lower_part, pads_low) + jnp.pad(upper_part, pads_high)


def per_device_body(right_side, stiffness, panels):
    cells_first = stiffness.shape[0]
    cells_second = stiffness.shape[1]
    stiff_lifted = jnp.broadcast_to(stiffness[None, None], (1, 3) + stiffness.shape)
    padded, stiff_wide, right_wide = with_halo_stacked((panels, stiff_lifted, right_side[None]), 1)
    ext_stiff = stiff_wide[0, 0]
    ext_right = right_wide[0]
    own_wide = jnp.pad(panels, ((0, 0), (0, 0), (1, 1), (1, 1), (0, 0)))
    diag_tile = coarse_tile(own_wide, panels, stiffness, 0, 0)
    tile_list = [
        coarse_tile(padded, panels, stiffness, shift_first, shift_second)
        for shift_first, shift_second in neighbours
    ]
    weights = damping / jnp.diagonal(diag_tile)

    def precondition(current, ext_residual=None):
        restricted = jnp.einsum("kabcd,abcd->k", panels, current, precision=precise)
        first_guess = weights * restricted
        if ext_residual is None:
            ext_residual = with_halo(current, (("gx", 1), ("gy", 2)), 1)
        correction = jacobi(ext_residual, ext_stiff)
        rows, cols = correction.shape[1], correction.shape[2]
        carrier = jnp.zeros((1,) + correction.shape[1:], correction.dtype)
        for row in (0, rows - 1):
            for col in (0, cols - 1):
                carrier = carrier.at[0, row, col, : first_guess.shape[0]].set(first_guess)
        spread_all = with_halo(
            jnp.concatenate([correction, carrier], axis=0), (("gx", 1), ("gy", 2)), 1
        )
        spread, carried = spread_all[:3], spread_all[3]
        place_row = {-1: 0, 0: 1, 1: rows + 1}
        place_col = {-1: 0, 0: 1, 1: cols + 1}
        applied = jnp.dot(diag_tile, first_guess, precision=precise)
        for place, (shift_first, shift_second) in enumerate(neighbours):
            guess = carried[place_row[shift_first], place_col[shift_second], : first_guess.shape[0]]
            applied = applied + jnp.dot(tile_list[place], guess, precision=precise)
        coarse_vec = first_guess + weights * (restricted - applied)
        coarse_part = jnp.einsum("k,kabcd->abcd", coarse_vec, panels, precision=precise)
        folded = fold_axis(fold_axis(spread, 1, cells_first), 2, cells_second)
        return folded + coarse_part

    def operate(field):
        return apply_stencil(with_halo(field, (("gx", 1), ("gy", 2)), 1), stiffness)

    residual = right_side
    precond = precondition(residual, ext_right)
    ext_imaged = apply_stencil(with_halo(precond, (("gx", 1), ("gy", 2)), 2), ext_stiff)
    ext_imaged = ext_imaged * inside_grid(cells_first, cells_second)
    imaged = ext_imaged[:, 1:-1, 1:-1, :]
    smoothed = precondition(imaged, ext_imaged)
    twice = operate(smoothed)
    local_dots = jnp.stack(
        [
            jnp.sum(residual * precond),
            jnp.sum(precond * imaged),
            jnp.sum(residual * smoothed),
            jnp.sum(imaged * smoothed),
            jnp.sum(smoothed * twice),
        ]
    )
    fit, curve, cross_r, cross_q, curve_w = butterfly_sum(local_dots, ("gx", "gy"))
    cross_z = cross_q
    step_first = fit / curve
    solution = step_first * precond
    residual = residual - step_first * imaged
    fit_next = fit - step_first * (curve + cross_r) + step_first * step_first * cross_q
    ratio = fit_next / fit
    grown = 1.0 + ratio
    curve_next = (
        grown * grown * curve
        - step_first * grown * (cross_z + cross_q)
        + step_first * step_first * curve_w
    )
    step_second = fit_next / curve_next
    precond_next = precond - step_first * smoothed
    direction = precond_next + ratio * precond
    imaged_next = (imaged - step_first * twice) + ratio * imaged
    solution = solution + step_second * direction
    residual = residual - step_second * imaged_next
    coupling = jnp.stack(tile_list).reshape(1, 1, 8, -1)
    return (solution, residual, coupling)


def solution(mesh):
    return jax.shard_map(
        per_device_body,
        mesh=mesh,
        in_specs=(P(None, "gx", "gy", None), P("gx", "gy", None), P(None, None, "gx", "gy", None)),
        out_specs=(P(None, "gx", "gy", None), P(None, "gx", "gy", None), P("gx", "gy", None, None)),
        check_vma=False,
    )
```
